256 devices in a mesh: pipe: 4 (over x), expert: 16 (over z, core), dp: 4 (over y).
Axes of the slice: x: 4, y: 4, z: 8, core: 2. Of those that a mesh axis runs over, the one named last changes fastest.
Arguments:
- inputs: bfloat16 [4, 8192, 4096], P('pipe', ('expert', 'dp')), may hold values from -6 to 6
- routes: int32 [4, 8192, 1], P('pipe', ('expert', 'dp')), may hold values from 0 to 15; in each aligned block of 128 rows (0 to 127, 128 to 255, ..., all dimensions but the last counted through in order) at most 10 rows name the same one
- router_scores: float32 [4, 8192, 8], P('pipe', ('expert', 'dp')), may hold values from -2 to 2
- cotangent: bfloat16 [4, 8192, 4096], P('pipe', ('expert', 'dp')), may hold values from -6 to 6
- w_gate: bfloat16 [4, 16, 768, 4096], P('pipe', 'expert', 'dp'), may hold values from -0.09375 to 0.09375
- w_up: bfloat16 [4, 16, 768, 4096], P('pipe', 'expert', 'dp'), may hold values from -0.09375 to 0.09375
- w_down: bfloat16 [4, 16, 768, 4096], P('pipe', 'expert', 'dp'), may hold values from -0.21875 to 0.21875
Outputs:
- score_grad: float32 [4, 8192, 8], P('pipe', ('expert', 'dp'))
- grad_prev: bfloat16 [4, 8192, 4096], P('pipe', ('expert', 'dp'))
- grad_gate: bfloat16 [4, 16, 768, 4096], P('pipe', 'expert', 'dp')
- grad_up: bfloat16 [4, 16, 768, 4096], P('pipe', 'expert', 'dp')
- grad_down: bfloat16 [4, 16, 768, 4096], P('pipe', 'expert', 'dp')
The draws below stay inside these ranges and needn't reach their ends.
Inputs may be any that keep to these rules, and one draw needn't show every extreme that they name: `routes`: among the 128 tokens of one device in one section (one block) no expert is named more than 10 times, and in every draw some block names some expert exactly 10 times. Every expert is named by some token.
All inputs are finite; a program needn't handle non-finite values.
Results may differ from the reference program's by a relative error of at most 0.02.
Values may be sent and summed in bfloat16 or wider, within the bound.
No kernel may reach another device: no remote copies, remote signals or barrier semaphores. Data moves between devices by JAX's collectives and lax.ppermute only.
A program may use at most 128 MiB of HBM per device.

```python
import math
import jax
import jax.numpy as jnp
import numpy as np
from jax import lax

D = 4096
HIDDEN_SIZE = 768
CHOSEN = 8
TOK_DEV = 128
EXPERTS = 16
CAP = 10
BLOCKS = 64
TOKENS = 8192
HID_SLICE = 192
N_PIPE = 4
N_DP = 4


def level_of(own_key, dims, cuts, smallest, top_value):
    loudness, own = 1.0, jax.random.fold_in(own_key, 6)
    for dim, blocks in cuts:
        draws = jnp.exp(jax.random.uniform(jax.random.fold_in(own, dim), (blocks,), jnp.float32, smallest / len(cuts), top_value / len(cuts)))
        loudness = loudness * jnp.repeat(draws, dims[dim] // blocks).reshape([-1 if axis == dim else 1 for axis in range(len(dims))])
    return loudness


def assign_block(rng, own, number, rows, count, top, bound, slope):
    sequence = jax.random.permutation(rng, count)
    heavy_load, ordinary = portions_of(count, rows * top, bound, slope, True), portions_of(count, rows * top, bound, slope, False)
    places = jnp.arange(count)

    def named(tallies, rotation):
        used = int((tallies > 0).sum())
        fixed = max(1, used // 4)
        shifted = fixed + (places - fixed + rotation * (used - fixed)) % max(1, count - fixed)
        return jnp.zeros((count,), jnp.int32).at[sequence[jnp.where(places < fixed, places, shifted)]].set(jnp.asarray(tallies, jnp.int32))

    tallies = jnp.where(number % 4 == 0, named(heavy_load, number // 4), named(ordinary, number - number // 4 - 1))
    mixed = jax.random.permutation(jax.random.fold_in(own, 3), count)
    source_of, sink = mixed[0:count // 2 * 2:2], mixed[1:count // 2 * 2:2]
    room = jnp.minimum(tallies[source_of] - 1, bound - tallies[sink]) // 2
    room = jnp.where((source_of == sequence[0]) | (sink == sequence[0]) | (tallies[sink] == 0), 0, jnp.maximum(room, 0))
    shifted = jax.random.randint(jax.random.fold_in(own, 4), (count // 2,), 0, 1 << 20) % (room + 1)
    tallies = tallies.at[source_of].add(-shifted).at[sink].add(shifted)
    labels = jnp.searchsorted(jnp.cumsum(tallies), jnp.arange(rows * top), side="right").astype(jnp.int32)
    listing = labels.reshape(top, rows).T
    listing = listing[jax.random.permutation(jax.random.fold_in(own, 1), rows)]
    rotation = jax.random.randint(jax.random.fold_in(own, 2), (rows, 1), 0, top)
    return jnp.take_along_axis(listing, (jnp.arange(top)[None, :] + rotation) % top, axis=1)


def portions_of(amount, total, limit, slope, full):
    portions = [(1 << 20) // math.isqrt(grade ** slope) + 1 for grade in range(1, amount + 1)]
    largest = limit if full else min(limit, max(-(-total // amount), total * portions[0] // sum(portions)))
    least = 1 if total - largest >= amount - 1 else 0
    counts, surplus = [largest] + [least] * (amount - 1), total - largest - least * (amount - 1)
    while surplus > 0:
        candidates = [i for i in range(1, amount) if counts[i] < largest] or [i for i in range(1, amount) if counts[i] < limit]
        whole, remaining = sum([portions[i] for i in candidates]), surplus
        for i in candidates:
            addition = min(limit - counts[i], max(1, remaining * portions[i] // whole), surplus)
            counts[i] = counts[i] + addition
            surplus = surplus - addition
    return np.array(counts)


def bell_draw(own_key, extent, scale, reach, pieces=(), kind=jnp.bfloat16):
    values = jax.random.normal(own_key, extent, jnp.float32) * scale
    if len(pieces) > 0:
        values = level_of(own_key, extent, pieces, -0.22, 0.18) * values
    return jnp.clip(values, min=-reach, max=reach).astype(kind)


def setup_inputs(seed: int = 0) -> dict:
    splits = jax.random.split(jax.random.key(seed), 8)
    inputs = bell_draw(splits[0], (N_PIPE, TOKENS, D), 1.0, 6.0, ((0, 4), (1, 64)))
    routes_keys = jax.random.split(jax.random.fold_in(splits[1], 1), N_PIPE * TOKENS // TOK_DEV)
    routes_turns = jax.random.permutation(jax.random.fold_in(splits[1], 3), N_PIPE * TOKENS // TOK_DEV)
    routes = jax.vmap(lambda own, number: assign_block(jax.random.fold_in(splits[1], 2), own, number, TOK_DEV, EXPERTS, 1, CAP, 2))(routes_keys, routes_turns).reshape((N_PIPE, TOKENS, 1))
    router_scores = jnp.clip(jax.random.uniform(splits[2], (N_PIPE, TOKENS, CHOSEN), jnp.float32, -2.0, 2.0) * level_of(splits[2], (N_PIPE, TOKENS, CHOSEN), ((0, 4), (1, 64)), -0.4, 0.0), -2.0, 2.0)
    cotangent = bell_draw(splits[3], (N_PIPE, TOKENS, D), 1.0, 6.0, ((0, 4), (1, 64)))
    w_gate = bell_draw(splits[4], (N_PIPE, EXPERTS, HIDDEN_SIZE, D), D ** -0.5, 0.09375, ((0, 4), (1, 16), (2, 4)))
    w_up = bell_draw(splits[5], (N_PIPE, EXPERTS, HIDDEN_SIZE, D), D ** -0.5, 0.09375, ((0, 4), (1, 16), (2, 4)))
    w_down = bell_draw(splits[6], (N_PIPE, EXPERTS, HIDDEN_SIZE, D), HIDDEN_SIZE ** -0.5, 0.21875, ((0, 4), (1, 16), (2, 4)))
    return dict(inputs=inputs, routes=routes, router_scores=router_scores, cotangent=cotangent, w_gate=w_gate, w_up=w_up, w_down=w_down)


def block_tables(route_col, score_rows):
    expert_ids = jnp.arange(EXPERTS, dtype=jnp.int32)
    onehot = (route_col[:, None] == expert_ids).astype(jnp.int32)
    earlier = (jnp.cumsum(onehot, axis=0) - onehot).astype(jnp.int32)
    slot = jnp.sum(onehot * earlier, axis=1).astype(jnp.int32)
    position = (route_col * CAP + slot).astype(jnp.int32)
    raised = jnp.exp(score_rows)
    weights = raised / jnp.sum(raised, axis=1, keepdims=True)
    gate = lax.optimization_barrier(weights[:, 0].astype(jnp.bfloat16)).astype(jnp.float32)
    table = (position[:, None] == jnp.arange(EXPERTS * CAP, dtype=jnp.int32)).astype(jnp.float32)
    return weights, gate, table


def expert_pass(operands):
    rows_x, rows_grad, gate_mat, up_mat, down_mat = operands
    feature_contract = (((1,), (1,)), ((), ()))
    gate_pre = lax.dot_general(rows_x, gate_mat, feature_contract, preferred_element_type=jnp.float32)
    up_pre = lax.dot_general(rows_x, up_mat, feature_contract, preferred_element_type=jnp.float32)
    gate_sig = jax.nn.sigmoid(gate_pre)
    activated = (gate_pre * gate_sig * up_pre).astype(jnp.bfloat16)
    running = jnp.zeros((rows_x.shape[0], D), jnp.float32)
    for member in range(N_DP):
        start_col = member * HID_SLICE
        stop_col = start_col + HID_SLICE
        partial_value = jnp.dot(activated[:, start_col:stop_col], down_mat[start_col:stop_col], preferred_element_type=jnp.float32).astype(jnp.bfloat16)
        running = running + lax.optimization_barrier(partial_value).astype(jnp.float32)
    rows_y = running.astype(jnp.bfloat16)
    hidden_grad = lax.dot_general(rows_grad, down_mat, feature_contract, preferred_element_type=jnp.float32)
    pre_gate = (hidden_grad * up_pre * gate_sig * (1.0 + gate_pre * (1.0 - gate_sig))).astype(jnp.bfloat16)
    pre_up = (hidden_grad * gate_pre * gate_sig).astype(jnp.bfloat16)
    rows_contract = (((0,), (0,)), ((), ()))
    grad_down = lax.dot_general(activated, rows_grad, rows_contract, preferred_element_type=jnp.float32).astype(jnp.bfloat16)
    grad_gate = lax.dot_general(pre_gate, rows_x, rows_contract, preferred_element_type=jnp.float32).astype(jnp.bfloat16)
    grad_up = lax.dot_general(pre_up, rows_x, rows_contract, preferred_element_type=jnp.float32).astype(jnp.bfloat16)
    running = jnp.zeros((rows_x.shape[0], D), jnp.float32)
    for member in range(N_DP):
        start_col = member * HID_SLICE
        stop_col = start_col + HID_SLICE
        partial_value = jnp.dot(pre_gate[:, start_col:stop_col], gate_mat[start_col:stop_col], preferred_element_type=jnp.float32)
        partial_value = partial_value + jnp.dot(pre_up[:, start_col:stop_col], up_mat[start_col:stop_col], preferred_element_type=jnp.float32)
        running = running + lax.optimization_barrier(partial_value.astype(jnp.bfloat16)).astype(jnp.float32)
    rows_dx = running.astype(jnp.bfloat16)
    return rows_y, rows_dx, grad_gate, grad_up, grad_down


def section_pass(tokens_in, route_rows, score_rows, upstream, gate_all, up_all, down_all):
    route_b = route_rows[:, 0].reshape(BLOCKS, TOK_DEV)
    score_b = score_rows.reshape(BLOCKS, TOK_DEV, CHOSEN)
    weights, gate, table = jax.vmap(block_tables)(route_b, score_b)
    tokens_b = tokens_in.reshape(BLOCKS, TOK_DEV, D).astype(jnp.float32)
    upstream_b = upstream.reshape(BLOCKS, TOK_DEV, D).astype(jnp.float32)

    def to_rows(values):
        return values.reshape(BLOCKS, EXPERTS, CAP, D).transpose(1, 0, 2, 3).reshape(EXPERTS, BLOCKS * CAP, D)

    def to_blocks(values):
        return values.reshape(EXPERTS, BLOCKS, CAP, D).transpose(1, 0, 2, 3).reshape(BLOCKS, EXPERTS * CAP, D).astype(jnp.float32)

    rows_x = to_rows(jnp.einsum('btp,btk->bpk', table, tokens_b)).astype(jnp.bfloat16)
    scaled = lax.optimization_barrier((gate[:, :, None] * upstream_b).astype(jnp.bfloat16)).astype(jnp.float32)
    rows_grad = to_rows(jnp.einsum('btp,btk->bpk', table, scaled)).astype(jnp.bfloat16)
    rows_y, rows_dx, grad_gate, grad_up, grad_down = lax.map(expert_pass, (rows_x, rows_grad, gate_all, up_all, down_all))
    blocks_y = to_blocks(rows_y)
    scores_grad = jnp.einsum('btk,bpk->btp', upstream_b, blocks_y)
    gate_grad = jnp.sum(table * scores_grad, axis=2)
    is_first = (jnp.arange(CHOSEN) == 0).astype(jnp.float32)
    score_grad = gate_grad[:, :, None] * weights[:, :, 0:1] * (is_first - weights)
    input_grad = jnp.einsum('btp,bpk->btk', table, to_blocks(rows_dx)).astype(jnp.bfloat16).reshape(TOKENS, D)
    return score_grad.reshape(TOKENS, CHOSEN), input_grad, grad_gate, grad_up, grad_down


def reference(inputs, routes, router_scores, cotangent, w_gate, w_up, w_down):
    results = []
    for section_id in range(N_PIPE):
        results.append(section_pass(inputs[section_id], routes[section_id], router_scores[section_id], cotangent[section_id], w_gate[section_id], w_up[section_id], w_down[section_id]))
    score_grad = jnp.stack([item[0] for item in results])
    handed = [item[1] for item in results[1:]] + [jnp.zeros((TOKENS, D), jnp.bfloat16)]
    grad_prev = jnp.stack(handed)
    grad_gate = jnp.stack([item[2] for item in results])
    grad_up = jnp.stack([item[3] for item in results])
    grad_down = jnp.stack([item[4] for item in results])
    return (score_grad, grad_prev, grad_gate, grad_up, grad_down)
```

```python
import jax
import jax.numpy as jnp
from jax import lax
from jax.sharding import PartitionSpec as P


def from_behind(shard, axis, by):
    length = lax.axis_size(axis)
    pairs = [(i, i + by) for i in range(length) if 0 <= i + by < length]
    return lax.ppermute(shard, axis, pairs)


def route_tables(route_col, score_rows, experts, capacity):
    expert_ids = jnp.arange(experts, dtype=jnp.int32)
    onehot = (route_col[:, None] == expert_ids).astype(jnp.int32)
    earlier = jnp.cumsum(onehot, axis=0) - onehot
    slot = jnp.sum(onehot * earlier, axis=1)
    position = route_col * capacity + slot
    raised = jnp.exp(score_rows)
    weights = raised / jnp.sum(raised, axis=1, keepdims=True)
    gate = lax.optimization_barrier(weights[:, 0].astype(jnp.bfloat16)).astype(jnp.float32)
    table = position[:, None] == jnp.arange(experts * capacity, dtype=jnp.int32)
    return (weights, gate, table)


def per_device(inputs, routes, router_scores, cotangent, w_gate, w_up, w_down):
    tokens_in = inputs[0]
    upstream = cotangent[0]
    route_col = routes[0][:, 0]
    score_rows = router_scores[0]
    gate_mat = w_gate[0, 0]
    up_mat = w_up[0, 0]
    down_mat = w_down[0, 0]
    experts = lax.axis_size("expert")
    groups = lax.axis_size("dp")
    token_count, model_width = tokens_in.shape
    capacity = max(2, token_count * 5 // (4 * experts))
    weights, gate, table = route_tables(route_col, score_rows, experts, capacity)
    table_half = table.astype(jnp.bfloat16)
    token_contract = (((0,), (0,)), ((), ()))
    feature_contract = (((1,), (1,)), ((), ()))
    local_x = lax.dot_general(
        table_half, tokens_in, token_contract, preferred_element_type=jnp.float32
    )
    local_x = local_x.astype(jnp.bfloat16).reshape(experts, capacity, model_width)
    local_up = lax.dot_general(
        table_half, upstream, token_contract, preferred_element_type=jnp.float32
    )
    local_up = local_up.astype(jnp.bfloat16).reshape(experts, capacity, model_width)
    local_gate = jnp.sum(jnp.where(table, gate[:, None], jnp.float32(0.0)), axis=0)
    local_gate = local_gate.astype(jnp.bfloat16).reshape(experts, capacity)
    x_e = lax.all_to_all(local_x, "expert", 0, 0, tiled=True)
    up_e = lax.all_to_all(local_up, "expert", 0, 0, tiled=True)
    gate_e = lax.all_to_all(local_gate, "expert", 0, 0, tiled=True)
    rows_x = lax.all_gather(x_e, "dp", axis=0, tiled=True).reshape(-1, model_width)
    rows_up = lax.all_gather(up_e, "dp", axis=0, tiled=True).reshape(-1, model_width)
    rows_gate = lax.all_gather(gate_e, "dp", axis=0, tiled=True).reshape(-1)
    rows_grad = (rows_gate.astype(jnp.float32)[:, None] * rows_up.astype(jnp.float32)).astype(
        jnp.bfloat16
    )
    gate_pre = lax.dot_general(
        rows_x, gate_mat, feature_contract, preferred_element_type=jnp.float32
    )
    up_pre = lax.dot_general(rows_x, up_mat, feature_contract, preferred_element_type=jnp.float32)
    gate_sig = jax.nn.sigmoid(gate_pre)
    activated = (gate_pre * gate_sig * up_pre).astype(jnp.bfloat16)
    partial_out = jnp.dot(activated, down_mat, preferred_element_type=jnp.float32)
    row_score = jnp.sum(partial_out * rows_up.astype(jnp.float32), axis=1)
    row_score = lax.psum_scatter(
        row_score.reshape(groups, experts, capacity), "dp", scatter_dimension=0, tiled=True
    ).reshape(experts, capacity)
    slot_score = lax.all_to_all(row_score, "expert", 0, 0, tiled=True).reshape(-1)
    gate_grad = jnp.sum(jnp.where(table, slot_score[None, :], jnp.float32(0.0)), axis=1)
    is_first = (jnp.arange(score_rows.shape[1]) == 0).astype(jnp.float32)
    score_grad = gate_grad[:, None] * weights[:, 0:1] * (is_first - weights)
    hidden_grad = lax.dot_general(
        rows_grad, down_mat, feature_contract, preferred_element_type=jnp.float32
    )
    pre_gate = (hidden_grad * up_pre * gate_sig * (1.0 + gate_pre * (1.0 - gate_sig))).astype(
        jnp.bfloat16
    )
    pre_up = (hidden_grad * gate_pre * gate_sig).astype(jnp.bfloat16)
    grad_down = lax.dot_general(
        activated, rows_grad, token_contract, preferred_element_type=jnp.float32
    ).astype(jnp.bfloat16)
    grad_gate = lax.dot_general(
        pre_gate, rows_x, token_contract, preferred_element_type=jnp.float32
    ).astype(jnp.bfloat16)
    grad_up = lax.dot_general(
        pre_up, rows_x, token_contract, preferred_element_type=jnp.float32
    ).astype(jnp.bfloat16)
    partial_in = jnp.dot(pre_gate, gate_mat, preferred_element_type=jnp.float32)
    partial_in = partial_in + jnp.dot(pre_up, up_mat, preferred_element_type=jnp.float32)
    outgoing = partial_in.astype(jnp.bfloat16).reshape(groups, experts, capacity, model_width)
    summed = lax.psum_scatter(outgoing, "dp", scatter_dimension=0, tiled=True)
    summed = summed.reshape(experts, capacity, model_width)
    flat_in = lax.all_to_all(summed, "expert", 0, 0, tiled=True).reshape(-1, model_width)
    input_grad = jnp.dot(table_half, flat_in, preferred_element_type=jnp.float32).astype(
        jnp.bfloat16
    )
    handed = from_behind(input_grad, "pipe", -1)
    return (
        score_grad[None],
        handed[None],
        grad_gate[None, None],
        grad_up[None, None],
        grad_down[None, None],
    )


def solution(mesh):
    in_specs = (
        P("pipe", ("expert", "dp"), None),
        P("pipe", ("expert", "dp"), None),
        P("pipe", ("expert", "dp"), None),
        P("pipe", ("expert", "dp"), None),
        P("pipe", "expert", "dp", None),
        P("pipe", "expert", "dp", None),
        P("pipe", "expert", "dp", None),
    )
    out_specs = (
        P("pipe", ("expert", "dp"), None),
        P("pipe", ("expert", "dp"), None),
        P("pipe", "expert", "dp", None),
        P("pipe", "expert", "dp", None),
        P("pipe", "expert", "dp", None),
    )
    return jax.shard_map(
        per_device, mesh=mesh, in_specs=in_specs, out_specs=out_specs, check_vma=False
    )
```

```python
import jax
import jax.numpy as jnp
from jax import lax
from jax.sharding import PartitionSpec as P


def from_behind(shard, axis, by):
    length = lax.axis_size(axis)
    pairs = [(i, i + by) for i in range(length) if 0 <= i + by < length]
    return lax.ppermute(shard, axis, pairs)


def route_tables(route_col, score_rows, experts, capacity):
    expert_ids = jnp.arange(experts, dtype=jnp.int32)
    onehot = (route_col[:, None] == expert_ids).astype(jnp.int32)
    earlier = jnp.cumsum(onehot, axis=0) - onehot
    slot = jnp.sum(onehot * earlier, axis=1)
    position = route_col * capacity + slot
    raised = jnp.exp(score_rows)
    weights = raised / jnp.sum(raised, axis=1, keepdims=True)
    gate = lax.optimization_barrier(weights[:, 0].astype(jnp.bfloat16)).astype(jnp.float32)
    table = position[:, None] == jnp.arange(experts * capacity, dtype=jnp.int32)
    return (weights, gate, table)


def dense_chunks(rows, chunks):
    return rows.reshape(chunks, -1, 1024)


def per_device(inputs, routes, router_scores, cotangent, w_gate, w_up, w_down):
    tokens_in = inputs[0]
    upstream = cotangent[0]
    route_col = routes[0][:, 0]
    score_rows = router_scores[0]
    gate_mat = w_gate[0, 0]
    up_mat = w_up[0, 0]
    down_mat = w_down[0, 0]
    experts = lax.axis_size("expert")
    groups = lax.axis_size("dp")
    my_expert = lax.axis_index("expert")
    my_group = lax.axis_index("dp")
    token_count, model_width = tokens_in.shape
    capacity = max(2, token_count * 5 // (4 * experts))
    weights, gate, table = route_tables(route_col, score_rows, experts, capacity)
    table_half = table.astype(jnp.bfloat16)
    token_contract = (((0,), (0,)), ((), ()))
    feature_contract = (((1,), (1,)), ((), ()))
    scaled = (gate[:, None] * upstream.astype(jnp.float32)).astype(jnp.bfloat16)
    local_x = lax.dot_general(
        table_half, tokens_in, token_contract, preferred_element_type=jnp.float32
    ).astype(jnp.bfloat16)
    local_dy = lax.dot_general(
        table_half, scaled, token_contract, preferred_element_type=jnp.float32
    ).astype(jnp.bfloat16)
    x_e = lax.all_to_all(dense_chunks(local_x, experts), "expert", 0, 0, tiled=True)
    x_e = x_e.reshape(experts * capacity, model_width)
    rows_x = lax.all_gather(x_e, "dp", axis=0, tiled=True)
    dy_e = lax.all_to_all(dense_chunks(local_dy, experts), "expert", 0, 0, tiled=True)
    dy_e = dy_e.reshape(experts * capacity, model_width)
    rows_grad = lax.all_gather(dy_e, "dp", axis=0, tiled=True)
    gate_pre = lax.dot_general(
        rows_x, gate_mat, feature_contract, preferred_element_type=jnp.float32
    )
    up_pre = lax.dot_general(rows_x, up_mat, feature_contract, preferred_element_type=jnp.float32)
    gate_sig = jax.nn.sigmoid(gate_pre)
    activated = (gate_pre * gate_sig * up_pre).astype(jnp.bfloat16)
    partial_out = jnp.dot(activated, down_mat, preferred_element_type=jnp.float32)
    row_score = jnp.sum(partial_out * rows_grad.astype(jnp.float32), axis=1)
    all_scores = lax.all_gather(row_score, ("expert", "dp"), axis=0, tiled=False)
    all_scores = jnp.sum(all_scores.reshape(experts, groups, -1), axis=1)
    all_scores = all_scores.reshape(experts, groups, experts, capacity)
    mine = lax.dynamic_index_in_dim(all_scores, my_group, axis=1, keepdims=False)
    mine = lax.dynamic_index_in_dim(mine, my_expert, axis=1, keepdims=False)
    slot_score = mine.reshape(-1)
    picked = jnp.sum(jnp.where(table, slot_score[None, :], jnp.float32(0.0)), axis=1)
    gate_grad = picked / gate
    is_first = (jnp.arange(score_rows.shape[1]) == 0).astype(jnp.float32)
    score_grad = gate_grad[:, None] * weights[:, 0:1] * (is_first - weights)
    hidden_grad = lax.dot_general(
        rows_grad, down_mat, feature_contract, preferred_element_type=jnp.float32
    )
    pre_gate = (hidden_grad * up_pre * gate_sig * (1.0 + gate_pre * (1.0 - gate_sig))).astype(
        jnp.bfloat16
    )
    pre_up = (hidden_grad * gate_pre * gate_sig).astype(jnp.bfloat16)
    grad_down = lax.dot_general(
        activated, rows_grad, token_contract, preferred_element_type=jnp.float32
    ).astype(jnp.bfloat16)
    grad_gate = lax.dot_general(
        pre_gate, rows_x, token_contract, preferred_element_type=jnp.float32
    ).astype(jnp.bfloat16)
    grad_up = lax.dot_general(
        pre_up, rows_x, token_contract, preferred_element_type=jnp.float32
    ).astype(jnp.bfloat16)
    partial_in = jnp.dot(pre_gate, gate_mat, preferred_element_type=jnp.float32)
    partial_in = partial_in + jnp.dot(pre_up, up_mat, preferred_element_type=jnp.float32)
    summed = lax.psum_scatter(partial_in.astype(jnp.bfloat16), "dp", scatter_dimension=0, tiled=True)
    back = lax.all_to_all(dense_chunks(summed, experts), "expert", 0, 0, tiled=True)
    flat_in = back.reshape(experts * capacity, model_width)
    input_grad = jnp.dot(table_half, flat_in, preferred_element_type=jnp.float32).astype(
        jnp.bfloat16
    )
    handed = from_behind(input_grad, "pipe", -1)
    return (
        score_grad[None],
        handed[None],
        grad_gate[None, None],
        grad_up[None, None],
        grad_down[None, None],
    )


def solution(mesh):
    in_specs = (
        P("pipe", ("expert", "dp"), None),
        P("pipe", ("expert", "dp"), None),
        P("pipe", ("expert", "dp"), None),
        P("pipe", ("expert", "dp"), None),
        P("pipe", "expert", "dp", None),
        P("pipe", "expert", "dp", None),
        P("pipe", "expert", "dp", None),
    )
    out_specs = (
        P("pipe", ("expert", "dp"), None),
        P("pipe", ("expert", "dp"), None),
        P("pipe", "expert", "dp", None),
        P("pipe", "expert", "dp", None),
        P("pipe", "expert", "dp", None),
    )
    return jax.shard_map(
        per_device, mesh=mesh, in_specs=in_specs, out_specs=out_specs, check_vma=False
    )
```

```python
import jax
import jax.numpy as jnp
from jax import lax
from jax.sharding import PartitionSpec as P


def from_behind(shard, axis, by):
    length = lax.axis_size(axis)
    pairs = [(i, i + by) for i in range(length) if 0 <= i + by < length]
    return lax.ppermute(shard, axis, pairs)


def route_tables(route_col, score_rows, experts, capacity):
    expert_ids = jnp.arange(experts, dtype=jnp.int32)
    onehot = (route_col[:, None] == expert_ids).astype(jnp.int32)
    earlier = jnp.cumsum(onehot, axis=0) - onehot
    slot = jnp.sum(onehot * earlier, axis=1)
    position = route_col * capacity + slot
    raised = jnp.exp(score_rows)
    weights = raised / jnp.sum(raised, axis=1, keepdims=True)
    gate = lax.optimization_barrier(weights[:, 0].astype(jnp.bfloat16)).astype(jnp.float32)
    table = position[:, None] == jnp.arange(experts * capacity, dtype=jnp.int32)
    return (weights, gate, table)


def dense_chunks(rows, chunks):
    return rows.reshape(chunks, -1, 1024)


def per_device(inputs, routes, router_scores, cotangent, w_gate, w_up, w_down):
    tokens_in = inputs[0]
    upstream = cotangent[0]
    route_col = routes[0][:, 0]
    score_rows = router_scores[0]
    gate_mat = w_gate[0, 0]
    up_mat = w_up[0, 0]
    down_mat = w_down[0, 0]
    experts = lax.axis_size("expert")
    groups = lax.axis_size("dp")
    my_expert = lax.axis_index("expert")
    my_group = lax.axis_index("dp")
    token_count, model_width = tokens_in.shape
    capacity = max(2, token_count * 5 // (4 * experts))
    weights, gate, table = route_tables(route_col, score_rows, experts, capacity)
    table_half = table.astype(jnp.bfloat16)
    token_contract = (((0,), (0,)), ((), ()))
    feature_contract = (((1,), (1,)), ((), ()))
    scaled = (gate[:, None] * upstream.astype(jnp.float32)).astype(jnp.bfloat16)
    local_x = lax.dot_general(
        table_half, tokens_in, token_contract, preferred_element_type=jnp.float32
    ).astype(jnp.bfloat16)
    local_dy = lax.dot_general(
        table_half, scaled, token_contract, preferred_element_type=jnp.float32
    ).astype(jnp.bfloat16)
    pieces = 2
    width = model_width // pieces
    rows_x = []
    rows_grad = []
    for q in range(pieces):
        cols = slice(q * width, (q + 1) * width)
        x_e = lax.all_to_all(dense_chunks(local_x[:, cols], experts), "expert", 0, 0, tiled=True)
        x_e = x_e.reshape(experts * capacity, width)
        rows_x.append(lax.all_gather(x_e, "dp", axis=0, tiled=True))
    for q in range(pieces):
        cols = slice(q * width, (q + 1) * width)
        dy_e = lax.all_to_all(dense_chunks(local_dy[:, cols], experts), "expert", 0, 0, tiled=True)
        dy_e = dy_e.reshape(experts * capacity, width)
        rows_grad.append(lax.all_gather(dy_e, "dp", axis=0, tiled=True))
    gate_pre = 0.0
    up_pre = 0.0
    for q in range(pieces):
        cols = slice(q * width, (q + 1) * width)
        gate_pre = gate_pre + lax.dot_general(
            rows_x[q], gate_mat[:, cols], feature_contract, preferred_element_type=jnp.float32
        )
        up_pre = up_pre + lax.dot_general(
            rows_x[q], up_mat[:, cols], feature_contract, preferred_element_type=jnp.float32
        )
    gate_sig = jax.nn.sigmoid(gate_pre)
    activated = (gate_pre * gate_sig * up_pre).astype(jnp.bfloat16)
    row_score = 0.0
    hidden_grad = 0.0
    for q in range(pieces):
        cols = slice(q * width, (q + 1) * width)
        partial_out = jnp.dot(activated, down_mat[:, cols], preferred_element_type=jnp.float32)
        row_score = row_score + jnp.sum(partial_out * rows_grad[q].astype(jnp.float32), axis=1)
        hidden_grad = hidden_grad + lax.dot_general(
            rows_grad[q], down_mat[:, cols], feature_contract, preferred_element_type=jnp.float32
        )
    row_score = lax.psum(row_score, "dp").reshape(groups, experts * capacity)
    row_score = lax.dynamic_index_in_dim(row_score, my_group, axis=0, keepdims=False)
    all_scores = lax.all_gather(row_score, "expert", axis=0, tiled=True)
    all_scores = all_scores.reshape(experts, experts, capacity)
    slot_score = lax.dynamic_index_in_dim(all_scores, my_expert, axis=1, keepdims=False)
    picked = jnp.sum(jnp.where(table, slot_score.reshape(-1)[None, :], jnp.float32(0.0)), axis=1)
    gate_grad = picked / gate
    is_first = (jnp.arange(score_rows.shape[1]) == 0).astype(jnp.float32)
    score_grad = gate_grad[:, None] * weights[:, 0:1] * (is_first - weights)
    pre_gate = (hidden_grad * up_pre * gate_sig * (1.0 + gate_pre * (1.0 - gate_sig))).astype(
        jnp.bfloat16
    )
    pre_up = (hidden_grad * gate_pre * gate_sig).astype(jnp.bfloat16)
    grad_down = []
    grad_gate = []
    grad_up = []
    grads_in = []
    for q in range(pieces):
        cols = slice(q * width, (q + 1) * width)
        grad_down.append(lax.dot_general(
            activated, rows_grad[q], token_contract, preferred_element_type=jnp.float32
        ).astype(jnp.bfloat16))
        grad_gate.append(lax.dot_general(
            pre_gate, rows_x[q], token_contract, preferred_element_type=jnp.float32
        ).astype(jnp.bfloat16))
        grad_up.append(lax.dot_general(
            pre_up, rows_x[q], token_contract, preferred_element_type=jnp.float32
        ).astype(jnp.bfloat16))
        partial_in = jnp.dot(pre_gate, gate_mat[:, cols], preferred_element_type=jnp.float32)
        partial_in = partial_in + jnp.dot(pre_up, up_mat[:, cols], preferred_element_type=jnp.float32)
        summed = lax.psum_scatter(
            partial_in.astype(jnp.bfloat16), "dp", scatter_dimension=0, tiled=True
        )
        back = lax.all_to_all(dense_chunks(summed, experts), "expert", 0, 0, tiled=True)
        flat_in = back.reshape(experts * capacity, width)
        grads_in.append(jnp.dot(table_half, flat_in, preferred_element_type=jnp.float32).astype(
            jnp.bfloat16
        ))
    grad_down = jnp.concatenate(grad_down, axis=1)
    grad_gate = jnp.concatenate(grad_gate, axis=1)
    grad_up = jnp.concatenate(grad_up, axis=1)
    input_grad = jnp.concatenate(grads_in, axis=1)
    handed = from_behind(input_grad, "pipe", -1)
    return (
        score_grad[None],
        handed[None],
        grad_gate[None, None],
        grad_up[None, None],
        grad_down[None, None],
    )


def solution(mesh):
    in_specs = (
        P("pipe", ("expert", "dp"), None),
        P("pipe", ("expert", "dp"), None),
        P("pipe", ("expert", "dp"), None),
        P("pipe", ("expert", "dp"), None),
        P("pipe", "expert", "dp", None),
        P("pipe", "expert", "dp", None),
        P("pipe", "expert", "dp", None),
    )
    out_specs = (
        P("pipe", ("expert", "dp"), None),
        P("pipe", ("expert", "dp"), None),
        P("pipe", "expert", "dp", None),
        P("pipe", "expert", "dp", None),
        P("pipe", "expert", "dp", None),
    )
    return jax.shard_map(
        per_device, mesh=mesh, in_specs=in_specs, out_specs=out_specs, check_vma=False
    )
```

```python
import jax
import jax.numpy as jnp
from jax import lax
from jax.sharding import PartitionSpec as P


def from_behind(shard, axis, by):
    length = lax.axis_size(axis)
    pairs = [(i, i + by) for i in range(length) if 0 <= i + by < length]
    return lax.ppermute(shard, axis, pairs)


def route_tables(route_col, score_rows, experts, capacity):
    expert_ids = jnp.arange(experts, dtype=jnp.int32)
    onehot = (route_col[:, None] == expert_ids).astype(jnp.int32)
    earlier = jnp.cumsum(onehot, axis=0) - onehot
    slot = jnp.sum(onehot * earlier, axis=1)
    position = route_col * capacity + slot
    raised = jnp.exp(score_rows)
    weights = raised / jnp.sum(raised, axis=1, keepdims=True)
    gate = lax.optimization_barrier(weights[:, 0].astype(jnp.bfloat16)).astype(jnp.float32)
    table = position[:, None] == jnp.arange(experts * capacity, dtype=jnp.int32)
    return (weights, gate, table)


def dense_chunks(rows, chunks):
    return rows.reshape(chunks, -1, 1024)


def per_device(inputs, routes, router_scores, cotangent, w_gate, w_up, w_down):
    tokens_in = inputs[0]
    upstream = cotangent[0]
    route_col = routes[0][:, 0]
    score_rows = router_scores[0]
    gate_mat = w_gate[0, 0]
    up_mat = w_up[0, 0]
    down_mat = w_down[0, 0]
    experts = lax.axis_size("expert")
    groups = lax.axis_size("dp")
    my_expert = lax.axis_index("expert")
    my_group = lax.axis_index("dp")
    token_count, model_width = tokens_in.shape
    capacity = max(2, token_count * 5 // (4 * experts))
    weights, gate, table = route_tables(route_col, score_rows, experts, capacity)
    table_half = table.astype(jnp.bfloat16)
    token_contract = (((0,), (0,)), ((), ()))
    feature_contract = (((1,), (1,)), ((), ()))
    scaled = (gate[:, None] * upstream.astype(jnp.float32)).astype(jnp.bfloat16)
    local_x = lax.dot_general(
        table_half, tokens_in, token_contract, preferred_element_type=jnp.float32
    ).astype(jnp.bfloat16)
    local_dy = lax.dot_general(
        table_half, scaled, token_contract, preferred_element_type=jnp.float32
    ).astype(jnp.bfloat16)
    pieces = 1
    width = model_width // pieces
    rows_x = []
    rows_grad = []
    for q in range(pieces):
        cols = slice(q * width, (q + 1) * width)
        x_e = lax.all_to_all(dense_chunks(local_x[:, cols], experts), "expert", 0, 0, tiled=True)
        x_e = x_e.reshape(experts * capacity, width)
        rows_x.append(lax.all_gather(x_e, "dp", axis=0, tiled=True))
    for q in range(pieces):
        cols = slice(q * width, (q + 1) * width)
        dy_e = lax.all_to_all(dense_chunks(local_dy[:, cols], experts), "expert", 0, 0, tiled=True)
        dy_e = dy_e.reshape(experts * capacity, width)
        rows_grad.append(lax.all_gather(dy_e, "dp", axis=0, tiled=True))
    gate_pre = 0.0
    up_pre = 0.0
    for q in range(pieces):
        cols = slice(q * width, (q + 1) * width)
        gate_pre = gate_pre + lax.dot_general(
            rows_x[q], gate_mat[:, cols], feature_contract, preferred_element_type=jnp.float32
        )
        up_pre = up_pre + lax.dot_general(
            rows_x[q], up_mat[:, cols], feature_contract, preferred_element_type=jnp.float32
        )
    gate_sig = jax.nn.sigmoid(gate_pre)
    activated = (gate_pre * gate_sig * up_pre).astype(jnp.bfloat16)
    row_score = 0.0
    hidden_grad = 0.0
    for q in range(pieces):
        cols = slice(q * width, (q + 1) * width)
        partial_out = jnp.dot(activated, down_mat[:, cols], preferred_element_type=jnp.float32)
        row_score = row_score + jnp.sum(partial_out * rows_grad[q].astype(jnp.float32), axis=1)
        hidden_grad = hidden_grad + lax.dot_general(
            rows_grad[q], down_mat[:, cols], feature_contract, preferred_element_type=jnp.float32
        )
    row_score = row_score.reshape(groups, experts, 1, capacity)
    onehot_e = (jnp.arange(experts) == my_expert).astype(jnp.float32)
    spread = row_score * onehot_e[None, None, :, None]
    spread = jnp.swapaxes(spread, 0, 1).reshape(experts * groups, experts, capacity)
    slot_score = lax.psum_scatter(spread, ("expert", "dp"), scatter_dimension=0, tiled=True)
    picked = jnp.sum(jnp.where(table, slot_score.reshape(-1)[None, :], jnp.float32(0.0)), axis=1)
    gate_grad = picked / gate
    is_first = (jnp.arange(score_rows.shape[1]) == 0).astype(jnp.float32)
    score_grad = gate_grad[:, None] * weights[:, 0:1] * (is_first - weights)
    pre_gate = (hidden_grad * up_pre * gate_sig * (1.0 + gate_pre * (1.0 - gate_sig))).astype(
        jnp.bfloat16
    )
    pre_up = (hidden_grad * gate_pre * gate_sig).astype(jnp.bfloat16)
    grad_down = []
    grad_gate = []
    grad_up = []
    grads_in = []
    for q in range(pieces):
        cols = slice(q * width, (q + 1) * width)
        grad_down.append(lax.dot_general(
            activated, rows_grad[q], token_contract, preferred_element_type=jnp.float32
        ).astype(jnp.bfloat16))
        grad_gate.append(lax.dot_general(
            pre_gate, rows_x[q], token_contract, preferred_element_type=jnp.float32
        ).astype(jnp.bfloat16))
        grad_up.append(lax.dot_general(
            pre_up, rows_x[q], token_contract, preferred_element_type=jnp.float32
        ).astype(jnp.bfloat16))
        partial_in = jnp.dot(pre_gate, gate_mat[:, cols], preferred_element_type=jnp.float32)
        partial_in = partial_in + jnp.dot(pre_up, up_mat[:, cols], preferred_element_type=jnp.float32)
        summed = lax.psum_scatter(
            partial_in.astype(jnp.bfloat16), "dp", scatter_dimension=0, tiled=True
        )
        back = lax.all_to_all(dense_chunks(summed, experts), "expert", 0, 0, tiled=True)
        flat_in = back.reshape(experts * capacity, width)
        grads_in.append(jnp.dot(table_half, flat_in, preferred_element_type=jnp.float32).astype(
            jnp.bfloat16
        ))
    grad_down = jnp.concatenate(grad_down, axis=1)
    grad_gate = jnp.concatenate(grad_gate, axis=1)
    grad_up = jnp.concatenate(grad_up, axis=1)
    input_grad = jnp.concatenate(grads_in, axis=1)
    handed = from_behind(input_grad, "pipe", -1)
    return (
        score_grad[None],
        handed[None],
        grad_gate[None, None],
        grad_up[None, None],
        grad_down[None, None],
    )


def solution(mesh):
    in_specs = (
        P("pipe", ("expert", "dp"), None),
        P("pipe", ("expert", "dp"), None),
        P("pipe", ("expert", "dp"), None),
        P("pipe", ("expert", "dp"), None),
        P("pipe", "expert", "dp", None),
        P("pipe", "expert", "dp", None),
        P("pipe", "expert", "dp", None),
    )
    out_specs = (
        P("pipe", ("expert", "dp"), None),
        P("pipe", ("expert", "dp"), None),
        P("pipe", "expert", "dp", None),
        P("pipe", "expert", "dp", None),
        P("pipe", "expert", "dp", None),
    )
    return jax.shard_map(
        per_device, mesh=mesh, in_specs=in_specs, out_specs=out_specs, check_vma=False
    )
```

```python
import jax
import jax.numpy as jnp
from jax import lax
from jax.sharding import PartitionSpec as P


def from_behind(shard, axis, by):
    length = lax.axis_size(axis)
    pairs = [(i, i + by) for i in range(length) if 0 <= i + by < length]
    return lax.ppermute(shard, axis, pairs)


def route_tables(route_col, score_rows, experts, capacity):
    expert_ids = jnp.arange(experts, dtype=jnp.int32)
    onehot = (route_col[:, None] == expert_ids).astype(jnp.int32)
    earlier = jnp.cumsum(onehot, axis=0) - onehot
    slot = jnp.sum(onehot * earlier, axis=1)
    position = route_col * capacity + slot
    raised = jnp.exp(score_rows)
    weights = raised / jnp.sum(raised, axis=1, keepdims=True)
    gate = lax.optimization_barrier(weights[:, 0].astype(jnp.bfloat16)).astype(jnp.float32)
    table = position[:, None] == jnp.arange(experts * capacity, dtype=jnp.int32)
    return (weights, gate, table)


def dense_chunks(rows, chunks):
    return rows.reshape(chunks, -1, 1024)


def per_device(inputs, routes, router_scores, cotangent, w_gate, w_up, w_down):
    tokens_in = inputs[0]
    upstream = cotangent[0]
    route_col = routes[0][:, 0]
    score_rows = router_scores[0]
    gate_mat = w_gate[0, 0]
    up_mat = w_up[0, 0]
    down_mat = w_down[0, 0]
    experts = lax.axis_size("expert")
    groups = lax.axis_size("dp")
    my_expert = lax.axis_index("expert")
    my_group = lax.axis_index("dp")
    token_count, model_width = tokens_in.shape
    capacity = max(2, token_count * 5 // (4 * experts))
    weights, gate, table = route_tables(route_col, score_rows, experts, capacity)
    table_half = table.astype(jnp.bfloat16)
    token_contract = (((0,), (0,)), ((), ()))
    feature_contract = (((1,), (1,)), ((), ()))
    scaled = (gate[:, None] * upstream.astype(jnp.float32)).astype(jnp.bfloat16)
    local_x = lax.dot_general(
        table_half, tokens_in, token_contract, preferred_element_type=jnp.float32
    ).astype(jnp.bfloat16)
    local_dy = lax.dot_general(
        table_half, scaled, token_contract, preferred_element_type=jnp.float32
    ).astype(jnp.bfloat16)
    pieces = 1
    width = model_width // pieces
    rows_x = []
    rows_grad = []
    for q in range(pieces):
        cols = slice(q * width, (q + 1) * width)
        x_e = lax.all_to_all(dense_chunks(local_x[:, cols], experts), "expert", 0, 0, tiled=True)
        x_e = x_e.reshape(experts * capacity, width)
        rows_x.append(lax.all_gather(x_e, "dp", axis=0, tiled=True))
    for q in range(pieces):
        cols = slice(q * width, (q + 1) * width)
        dy_e = lax.all_to_all(dense_chunks(local_dy[:, cols], experts), "expert", 0, 0, tiled=True)
        dy_e = dy_e.reshape(experts * capacity, width)
        rows_grad.append(lax.all_gather(dy_e, "dp", axis=0, tiled=True))
    gate_pre = 0.0
    up_pre = 0.0
    for q in range(pieces):
        cols = slice(q * width, (q + 1) * width)
        gate_pre = gate_pre + lax.dot_general(
            rows_x[q], gate_mat[:, cols], feature_contract, preferred_element_type=jnp.float32
        )
        up_pre = up_pre + lax.dot_general(
            rows_x[q], up_mat[:, cols], feature_contract, preferred_element_type=jnp.float32
        )
    gate_sig = jax.nn.sigmoid(gate_pre)
    activated = (gate_pre * gate_sig * up_pre).astype(jnp.bfloat16)
    row_score = 0.0
    hidden_grad = 0.0
    for q in range(pieces):
        cols = slice(q * width, (q + 1) * width)
        partial_out = jnp.dot(activated, down_mat[:, cols], preferred_element_type=jnp.float32)
        row_score = row_score + jnp.sum(partial_out * rows_grad[q].astype(jnp.float32), axis=1)
        hidden_grad = hidden_grad + lax.dot_general(
            rows_grad[q], down_mat[:, cols], feature_contract, preferred_element_type=jnp.float32
        )
    pre_gate = (hidden_grad * up_pre * gate_sig * (1.0 + gate_pre * (1.0 - gate_sig))).astype(
        jnp.bfloat16
    )
    pre_up = (hidden_grad * gate_pre * gate_sig).astype(jnp.bfloat16)
    grad_down = []
    grad_gate = []
    grad_up = []
    grads_in = []
    for q in range(pieces):
        cols = slice(q * width, (q + 1) * width)
        grad_down.append(lax.dot_general(
            activated, rows_grad[q], token_contract, preferred_element_type=jnp.float32
        ).astype(jnp.bfloat16))
        grad_gate.append(lax.dot_general(
            pre_gate, rows_x[q], token_contract, preferred_element_type=jnp.float32
        ).astype(jnp.bfloat16))
        grad_up.append(lax.dot_general(
            pre_up, rows_x[q], token_contract, preferred_element_type=jnp.float32
        ).astype(jnp.bfloat16))
        partial_in = jnp.dot(pre_gate, gate_mat[:, cols], preferred_element_type=jnp.float32)
        partial_in = partial_in + jnp.dot(pre_up, up_mat[:, cols], preferred_element_type=jnp.float32)
        score_cols = jnp.pad(row_score[:, None], ((0, 0), (0, 127)))
        outgoing = jnp.concatenate([partial_in, score_cols], axis=1).astype(jnp.bfloat16)
        summed = lax.psum_scatter(outgoing, "dp", scatter_dimension=0, tiled=True)
        body = summed[:, :width].reshape(experts, 8, capacity * width // 8)
        tail = summed[:, width].reshape(experts, 1, capacity)
        tail = jnp.pad(tail, ((0, 0), (0, 7), (0, 128 - capacity)))
        back = lax.all_to_all(jnp.concatenate([body, tail], axis=2), "expert", 0, 0, tiled=True)
        flat_in = back[:, :, : capacity * width // 8].reshape(experts * capacity, width)
        slot_score = back[:, 0, capacity * width // 8 : capacity * width // 8 + capacity]
        grads_in.append(jnp.dot(table_half, flat_in, preferred_element_type=jnp.float32).astype(
            jnp.bfloat16
        ))
    grad_down = jnp.concatenate(grad_down, axis=1)
    grad_gate = jnp.concatenate(grad_gate, axis=1)
    grad_up = jnp.concatenate(grad_up, axis=1)
    input_grad = jnp.concatenate(grads_in, axis=1)
    slot_score = slot_score.astype(jnp.float32).reshape(-1)
    picked = jnp.sum(jnp.where(table, slot_score[None, :], jnp.float32(0.0)), axis=1)
    gate_grad = picked / gate
    is_first = (jnp.arange(score_rows.shape[1]) == 0).astype(jnp.float32)
    score_grad = gate_grad[:, None] * weights[:, 0:1] * (is_first - weights)
    handed = from_behind(input_grad, "pipe", -1)
    return (
        score_grad[None],
        handed[None],
        grad_gate[None, None],
        grad_up[None, None],
        grad_down[None, None],
    )


def solution(mesh):
    in_specs = (
        P("pipe", ("expert", "dp"), None),
        P("pipe", ("expert", "dp"), None),
        P("pipe", ("expert", "dp"), None),
        P("pipe", ("expert", "dp"), None),
        P("pipe", "expert", "dp", None),
        P("pipe", "expert", "dp", None),
        P("pipe", "expert", "dp", None),
    )
    out_specs = (
        P("pipe", ("expert", "dp"), None),
        P("pipe", ("expert", "dp"), None),
        P("pipe", "expert", "dp", None),
        P("pipe", "expert", "dp", None),
        P("pipe", "expert", "dp", None),
    )
    return jax.shard_map(
        per_device, mesh=mesh, in_specs=in_specs, out_specs=out_specs, check_vma=False
    )
```

```python
import jax
import jax.numpy as jnp
from jax import lax
from jax.sharding import PartitionSpec as P


def from_behind(shard, axis, by):
    length = lax.axis_size(axis)
    pairs = [(i, i + by) for i in range(length) if 0 <= i + by < length]
    return lax.ppermute(shard, axis, pairs)


def route_tables(route_col, score_rows, experts, capacity):
    expert_ids = jnp.arange(experts, dtype=jnp.int32)
    onehot = (route_col[:, None] == expert_ids).astype(jnp.int32)
    earlier = jnp.cumsum(onehot, axis=0) - onehot
    slot = jnp.sum(onehot * earlier, axis=1)
    position = route_col * capacity + slot
    raised = jnp.exp(score_rows)
    weights = raised / jnp.sum(raised, axis=1, keepdims=True)
    gate = lax.optimization_barrier(weights[:, 0].astype(jnp.bfloat16)).astype(jnp.float32)
    table = position[:, None] == jnp.arange(experts * capacity, dtype=jnp.int32)
    return (weights, gate, table)


def dense_chunks(rows, chunks):
    return rows.reshape(chunks, -1, 1024)


def per_device(inputs, routes, router_scores, cotangent, w_gate, w_up, w_down):
    tokens_in = inputs[0]
    upstream = cotangent[0]
    route_col = routes[0][:, 0]
    score_rows = router_scores[0]
    gate_mat = w_gate[0, 0]
    up_mat = w_up[0, 0]
    down_mat = w_down[0, 0]
    experts = lax.axis_size("expert")
    groups = lax.axis_size("dp")
    my_expert = lax.axis_index("expert")
    my_group = lax.axis_index("dp")
    token_count, model_width = tokens_in.shape
    capacity = max(2, token_count * 5 // (4 * experts))
    weights, gate, table = route_tables(route_col, score_rows, experts, capacity)
    table_half = table.astype(jnp.bfloat16)
    token_contract = (((0,), (0,)), ((), ()))
    feature_contract = (((1,), (1,)), ((), ()))
    scaled = (gate[:, None] * upstream.astype(jnp.float32)).astype(jnp.bfloat16)
    local_x = lax.dot_general(
        table_half, tokens_in, token_contract, preferred_element_type=jnp.float32
    ).astype(jnp.bfloat16)
    local_dy = lax.dot_general(
        table_half, scaled, token_contract, preferred_element_type=jnp.float32
    ).astype(jnp.bfloat16)
    pieces = 1
    width = model_width // pieces
    rows_x = []
    rows_grad = []
    for q in range(pieces):
        cols = slice(q * width, (q + 1) * width)
        x_e = lax.all_to_all(dense_chunks(local_x[:, cols], experts), "expert", 0, 0, tiled=True)
        x_e = x_e.reshape(experts * capacity, width)
        whole = jnp.zeros((groups * experts * capacity, width), x_e.dtype)
        for shift in range(groups):
            if shift == 0:
                got = x_e
            else:
                pairs = [(k, (k + shift) % groups) for k in range(groups)]
                got = lax.ppermute(x_e, "dp", pairs)
            origin = (my_group - shift) % groups
            whole = lax.dynamic_update_slice_in_dim(whole, got, origin * experts * capacity, 0)
        rows_x.append(whole)
    for q in range(pieces):
        cols = slice(q * width, (q + 1) * width)
        dy_e = lax.all_to_all(dense_chunks(local_dy[:, cols], experts), "expert", 0, 0, tiled=True)
        dy_e = dy_e.reshape(experts * capacity, width)
        rows_grad.append(lax.all_gather(dy_e, "dp", axis=0, tiled=True))
    gate_pre = 0.0
    up_pre = 0.0
    for q in range(pieces):
        cols = slice(q * width, (q + 1) * width)
        gate_pre = gate_pre + lax.dot_general(
            rows_x[q], gate_mat[:, cols], feature_contract, preferred_element_type=jnp.float32
        )
        up_pre = up_pre + lax.dot_general(
            rows_x[q], up_mat[:, cols], feature_contract, preferred_element_type=jnp.float32
        )
    gate_sig = jax.nn.sigmoid(gate_pre)
    activated = (gate_pre * gate_sig * up_pre).astype(jnp.bfloat16)
    row_score = 0.0
    hidden_grad = 0.0
    for q in range(pieces):
        cols = slice(q * width, (q + 1) * width)
        partial_out = jnp.dot(activated, down_mat[:, cols], preferred_element_type=jnp.float32)
        row_score = row_score + jnp.sum(partial_out * rows_grad[q].astype(jnp.float32), axis=1)
        hidden_grad = hidden_grad + lax.dot_general(
            rows_grad[q], down_mat[:, cols], feature_contract, preferred_element_type=jnp.float32
        )
    pre_gate = (hidden_grad * up_pre * gate_sig * (1.0 + gate_pre * (1.0 - gate_sig))).astype(
        jnp.bfloat16
    )
    pre_up = (hidden_grad * gate_pre * gate_sig).astype(jnp.bfloat16)
    grad_down = []
    grad_gate = []
    grad_up = []
    grads_in = []
    for q in range(pieces):
        cols = slice(q * width, (q + 1) * width)
        grad_down.append(lax.dot_general(
            activated, rows_grad[q], token_contract, preferred_element_type=jnp.float32
        ).astype(jnp.bfloat16))
        grad_gate.append(lax.dot_general(
            pre_gate, rows_x[q], token_contract, preferred_element_type=jnp.float32
        ).astype(jnp.bfloat16))
        grad_up.append(lax.dot_general(
            pre_up, rows_x[q], token_contract, preferred_element_type=jnp.float32
        ).astype(jnp.bfloat16))
        partial_in = jnp.dot(pre_gate, gate_mat[:, cols], preferred_element_type=jnp.float32)
        partial_in = partial_in + jnp.dot(pre_up, up_mat[:, cols], preferred_element_type=jnp.float32)
        score_cols = jnp.pad(row_score[:, None], ((0, 0), (0, 127)))
        outgoing = jnp.concatenate([partial_in, score_cols], axis=1).astype(jnp.bfloat16)
        summed = lax.psum_scatter(outgoing, "dp", scatter_dimension=0, tiled=True)
        body = summed[:, :width].reshape(experts, 8, capacity * width // 8)
        tail = summed[:, width].reshape(experts, 1, capacity)
        tail = jnp.pad(tail, ((0, 0), (0, 7), (0, 128 - capacity)))
        back = lax.all_to_all(jnp.concatenate([body, tail], axis=2), "expert", 0, 0, tiled=True)
        flat_in = back[:, :, : capacity * width // 8].reshape(experts * capacity, width)
        slot_score = back[:, 0, capacity * width // 8 : capacity * width // 8 + capacity]
        grads_in.append(jnp.dot(table_half, flat_in, preferred_element_type=jnp.float32).astype(
            jnp.bfloat16
        ))
    grad_down = jnp.concatenate(grad_down, axis=1)
    grad_gate = jnp.concatenate(grad_gate, axis=1)
    grad_up = jnp.concatenate(grad_up, axis=1)
    input_grad = jnp.concatenate(grads_in, axis=1)
    slot_score = slot_score.astype(jnp.float32).reshape(-1)
    picked = jnp.sum(jnp.where(table, slot_score[None, :], jnp.float32(0.0)), axis=1)
    gate_grad = picked / gate
    is_first = (jnp.arange(score_rows.shape[1]) == 0).astype(jnp.float32)
    score_grad = gate_grad[:, None] * weights[:, 0:1] * (is_first - weights)
    handed = from_behind(input_grad, "pipe", -1)
    return (
        score_grad[None],
        handed[None],
        grad_gate[None, None],
        grad_up[None, None],
        grad_down[None, None],
    )


def solution(mesh):
    in_specs = (
        P("pipe", ("expert", "dp"), None),
        P("pipe", ("expert", "dp"), None),
        P("pipe", ("expert", "dp"), None),
        P("pipe", ("expert", "dp"), None),
        P("pipe", "expert", "dp", None),
        P("pipe", "expert", "dp", None),
        P("pipe", "expert", "dp", None),
    )
    out_specs = (
        P("pipe", ("expert", "dp"), None),
        P("pipe", ("expert", "dp"), None),
        P("pipe", "expert", "dp", None),
        P("pipe", "expert", "dp", None),
        P("pipe", "expert", "dp", None),
    )
    return jax.shard_map(
        per_device, mesh=mesh, in_specs=in_specs, out_specs=out_specs, check_vma=False
    )
```

```python
import jax
import jax.numpy as jnp
from jax import lax
from jax.sharding import PartitionSpec as P


def from_behind(shard, axis, by):
    length = lax.axis_size(axis)
    pairs = [(i, i + by) for i in range(length) if 0 <= i + by < length]
    return lax.ppermute(shard, axis, pairs)


def ring_gather(piece, axis, me):
    size = lax.axis_size(axis)
    rows = piece.shape[0]
    half = rows // 2
    fwd = [(k, (k + 1) % size) for k in range(size)]
    bwd = [(k, (k - 1) % size) for k in range(size)]
    from_left = lax.ppermute(piece, axis, fwd)
    from_right = lax.ppermute(piece, axis, bwd)
    far_top = lax.ppermute(from_left[:half], axis, fwd)
    far_bottom = lax.ppermute(from_right[half:], axis, bwd)
    whole = jnp.zeros((size * rows,) + piece.shape[1:], piece.dtype)
    whole = lax.dynamic_update_slice_in_dim(whole, piece, me * rows, 0)
    whole = lax.dynamic_update_slice_in_dim(whole, from_left, ((me - 1) % size) * rows, 0)
    whole = lax.dynamic_update_slice_in_dim(whole, from_right, ((me + 1) % size) * rows, 0)
    far = jnp.concatenate([far_top, far_bottom], axis=0)
    whole = lax.dynamic_update_slice_in_dim(whole, far, ((me + 2) % size) * rows, 0)
    return whole


def ring_reduce_scatter(parts, axis, me):
    size = lax.axis_size(axis)
    rows = parts.shape[0] // size
    half = rows // 2
    fwd = [(k, (k + 1) % size) for k in range(size)]
    bwd = [(k, (k - 1) % size) for k in range(size)]

    def block(t):
        return lax.dynamic_slice_in_dim(parts, (t % size) * rows, rows, 0)

    far = block(me + 2)
    got_top = lax.ppermute(far[:half], axis, fwd)
    got_bottom = lax.ppermute(far[half:], axis, bwd)
    to_right = block(me + 1).astype(jnp.float32)
    to_right = jnp.concatenate([to_right[:half] + got_top.astype(jnp.float32), to_right[half:]])
    to_left = block(me - 1).astype(jnp.float32)
    to_left = jnp.concatenate([to_left[:half], to_left[half:] + got_bottom.astype(jnp.float32)])
    from_left = lax.ppermute(to_right.astype(jnp.bfloat16), axis, fwd)
    from_right = lax.ppermute(to_left.astype(jnp.bfloat16), axis, bwd)
    total = block(me).astype(jnp.float32) + from_left.astype(jnp.float32)
    total = total + from_right.astype(jnp.float32)
    return total.astype(jnp.bfloat16)


def route_tables(route_col, score_rows, experts, capacity):
    expert_ids = jnp.arange(experts, dtype=jnp.int32)
    onehot = (route_col[:, None] == expert_ids).astype(jnp.int32)
    earlier = jnp.cumsum(onehot, axis=0) - onehot
    slot = jnp.sum(onehot * earlier, axis=1)
    position = route_col * capacity + slot
    raised = jnp.exp(score_rows)
    weights = raised / jnp.sum(raised, axis=1, keepdims=True)
    gate = lax.optimization_barrier(weights[:, 0].astype(jnp.bfloat16)).astype(jnp.float32)
    table = position[:, None] == jnp.arange(experts * capacity, dtype=jnp.int32)
    return (weights, gate, table)


def dense_chunks(rows, chunks):
    return rows.reshape(chunks, -1, 1024)


def per_device(inputs, routes, router_scores, cotangent, w_gate, w_up, w_down):
    tokens_in = inputs[0]
    upstream = cotangent[0]
    route_col = routes[0][:, 0]
    score_rows = router_scores[0]
    gate_mat = w_gate[0, 0]
    up_mat = w_up[0, 0]
    down_mat = w_down[0, 0]
    experts = lax.axis_size("expert")
    groups = lax.axis_size("dp")
    my_expert = lax.axis_index("expert")
    my_group = lax.axis_index("dp")
    token_count, model_width = tokens_in.shape
    capacity = max(2, token_count * 5 // (4 * experts))
    weights, gate, table = route_tables(route_col, score_rows, experts, capacity)
    table_half = table.astype(jnp.bfloat16)
    token_contract = (((0,), (0,)), ((), ()))
    feature_contract = (((1,), (1,)), ((), ()))
    scaled = (gate[:, None] * upstream.astype(jnp.float32)).astype(jnp.bfloat16)
    local_x = lax.dot_general(
        table_half, tokens_in, token_contract, preferred_element_type=jnp.float32
    ).astype(jnp.bfloat16)
    local_dy = lax.dot_general(
        table_half, scaled, token_contract, preferred_element_type=jnp.float32
    ).astype(jnp.bfloat16)
    pieces = 1
    width = model_width // pieces
    rows_x = []
    rows_grad = []
    for q in range(pieces):
        cols = slice(q * width, (q + 1) * width)
        x_e = lax.all_to_all(dense_chunks(local_x[:, cols], experts), "expert", 0, 0, tiled=True)
        x_e = x_e.reshape(experts * capacity, width)
        rows_x.append(ring_gather(x_e, "dp", my_group))
    for q in range(pieces):
        cols = slice(q * width, (q + 1) * width)
        dy_e = lax.all_to_all(dense_chunks(local_dy[:, cols], experts), "expert", 0, 0, tiled=True)
        dy_e = dy_e.reshape(experts * capacity, width)
        rows_grad.append(ring_gather(dy_e, "dp", my_group))
    gate_pre = 0.0
    up_pre = 0.0
    for q in range(pieces):
        cols = slice(q * width, (q + 1) * width)
        gate_pre = gate_pre + lax.dot_general(
            rows_x[q], gate_mat[:, cols], feature_contract, preferred_element_type=jnp.float32
        )
        up_pre = up_pre + lax.dot_general(
            rows_x[q], up_mat[:, cols], feature_contract, preferred_element_type=jnp.float32
        )
    gate_sig = jax.nn.sigmoid(gate_pre)
    activated = (gate_pre * gate_sig * up_pre).astype(jnp.bfloat16)
    row_score = 0.0
    hidden_grad = 0.0
    for q in range(pieces):
        cols = slice(q * width, (q + 1) * width)
        partial_out = jnp.dot(activated, down_mat[:, cols], preferred_element_type=jnp.float32)
        row_score = row_score + jnp.sum(partial_out * rows_grad[q].astype(jnp.float32), axis=1)
        hidden_grad = hidden_grad + lax.dot_general(
            rows_grad[q], down_mat[:, cols], feature_contract, preferred_element_type=jnp.float32
        )
    pre_gate = (hidden_grad * up_pre * gate_sig * (1.0 + gate_pre * (1.0 - gate_sig))).astype(
        jnp.bfloat16
    )
    pre_up = (hidden_grad * gate_pre * gate_sig).astype(jnp.bfloat16)
    grad_down = []
    grad_gate = []
    grad_up = []
    grads_in = []
    for q in range(pieces):
        cols = slice(q * width, (q + 1) * width)
        grad_down.append(lax.dot_general(
            activated, rows_grad[q], token_contract, preferred_element_type=jnp.float32
        ).astype(jnp.bfloat16))
        grad_gate.append(lax.dot_general(
            pre_gate, rows_x[q], token_contract, preferred_element_type=jnp.float32
        ).astype(jnp.bfloat16))
        grad_up.append(lax.dot_general(
            pre_up, rows_x[q], token_contract, preferred_element_type=jnp.float32
        ).astype(jnp.bfloat16))
        partial_in = jnp.dot(pre_gate, gate_mat[:, cols], preferred_element_type=jnp.float32)
        partial_in = partial_in + jnp.dot(pre_up, up_mat[:, cols], preferred_element_type=jnp.float32)
        score_cols = jnp.pad(row_score[:, None], ((0, 0), (0, 127)))
        outgoing = jnp.concatenate([partial_in, score_cols], axis=1).astype(jnp.bfloat16)
        summed = ring_reduce_scatter(outgoing, "dp", my_group)
        body = summed[:, :width].reshape(experts, 8, capacity * width // 8)
        tail = summed[:, width].reshape(experts, 1, capacity)
        tail = jnp.pad(tail, ((0, 0), (0, 7), (0, 128 - capacity)))
        back = lax.all_to_all(jnp.concatenate([body, tail], axis=2), "expert", 0, 0, tiled=True)
        flat_in = back[:, :, : capacity * width // 8].reshape(experts * capacity, width)
        slot_score = back[:, 0, capacity * width // 8 : capacity * width // 8 + capacity]
        grads_in.append(jnp.dot(table_half, flat_in, preferred_element_type=jnp.float32).astype(
            jnp.bfloat16
        ))
    grad_down = jnp.concatenate(grad_down, axis=1)
    grad_gate = jnp.concatenate(grad_gate, axis=1)
    grad_up = jnp.concatenate(grad_up, axis=1)
    input_grad = jnp.concatenate(grads_in, axis=1)
    slot_score = slot_score.astype(jnp.float32).reshape(-1)
    picked = jnp.sum(jnp.where(table, slot_score[None, :], jnp.float32(0.0)), axis=1)
    gate_grad = picked / gate
    is_first = (jnp.arange(score_rows.shape[1]) == 0).astype(jnp.float32)
    score_grad = gate_grad[:, None] * weights[:, 0:1] * (is_first - weights)
    handed = from_behind(input_grad, "pipe", -1)
    return (
        score_grad[None],
        handed[None],
        grad_gate[None, None],
        grad_up[None, None],
        grad_down[None, None],
    )


def solution(mesh):
    in_specs = (
        P("pipe", ("expert", "dp"), None),
        P("pipe", ("expert", "dp"), None),
        P("pipe", ("expert", "dp"), None),
        P("pipe", ("expert", "dp"), None),
        P("pipe", "expert", "dp", None),
        P("pipe", "expert", "dp", None),
        P("pipe", "expert", "dp", None),
    )
    out_specs = (
        P("pipe", ("expert", "dp"), None),
        P("pipe", ("expert", "dp"), None),
        P("pipe", "expert", "dp", None),
        P("pipe", "expert", "dp", None),
        P("pipe", "expert", "dp", None),
    )
    return jax.shard_map(
        per_device, mesh=mesh, in_specs=in_specs, out_specs=out_specs, check_vma=False
    )
```

```python
import jax
import jax.numpy as jnp
from jax import lax
from jax.sharding import PartitionSpec as P


def from_behind(shard, axis, by):
    length = lax.axis_size(axis)
    pairs = [(i, i + by) for i in range(length) if 0 <= i + by < length]
    return lax.ppermute(shard, axis, pairs)


def ring_gather(piece, axis, me):
    size = lax.axis_size(axis)
    rows = piece.shape[0]
    half = rows // 2
    fwd = [(k, (k + 1) % size) for k in range(size)]
    bwd = [(k, (k - 1) % size) for k in range(size)]
    from_left = lax.ppermute(piece, axis, fwd)
    from_right = lax.ppermute(piece, axis, bwd)
    far_top = lax.ppermute(from_left[:half], axis, fwd)
    far_bottom = lax.ppermute(from_right[half:], axis, bwd)
    whole = jnp.zeros((size * rows,) + piece.shape[1:], piece.dtype)
    whole = lax.dynamic_update_slice_in_dim(whole, piece, me * rows, 0)
    whole = lax.dynamic_update_slice_in_dim(whole, from_left, ((me - 1) % size) * rows, 0)
    whole = lax.dynamic_update_slice_in_dim(whole, from_right, ((me + 1) % size) * rows, 0)
    far = jnp.concatenate([far_top, far_bottom], axis=0)
    whole = lax.dynamic_update_slice_in_dim(whole, far, ((me + 2) % size) * rows, 0)
    return whole


def ring_reduce_scatter(parts, axis, me):
    size = lax.axis_size(axis)
    rows = parts.shape[0] // size
    half = rows // 2
    fwd = [(k, (k + 1) % size) for k in range(size)]
    bwd = [(k, (k - 1) % size) for k in range(size)]

    def block(t):
        return lax.dynamic_slice_in_dim(parts, (t % size) * rows, rows, 0)

    far = block(me + 2)
    got_top = lax.ppermute(far[:half], axis, fwd)
    got_bottom = lax.ppermute(far[half:], axis, bwd)
    to_right = block(me + 1).astype(jnp.float32)
    to_right = jnp.concatenate([to_right[:half] + got_top.astype(jnp.float32), to_right[half:]])
    to_left = block(me - 1).astype(jnp.float32)
    to_left = jnp.concatenate([to_left[:half], to_left[half:] + got_bottom.astype(jnp.float32)])
    from_left = lax.ppermute(to_right.astype(jnp.bfloat16), axis, fwd)
    from_right = lax.ppermute(to_left.astype(jnp.bfloat16), axis, bwd)
    total = block(me).astype(jnp.float32) + from_left.astype(jnp.float32)
    total = total + from_right.astype(jnp.float32)
    return total.astype(jnp.bfloat16)


def route_tables(route_col, score_rows, experts, capacity):
    expert_ids = jnp.arange(experts, dtype=jnp.int32)
    onehot = (route_col[:, None] == expert_ids).astype(jnp.int32)
    earlier = jnp.cumsum(onehot, axis=0) - onehot
    slot = jnp.sum(onehot * earlier, axis=1)
    position = route_col * capacity + slot
    raised = jnp.exp(score_rows)
    weights = raised / jnp.sum(raised, axis=1, keepdims=True)
    gate = lax.optimization_barrier(weights[:, 0].astype(jnp.bfloat16)).astype(jnp.float32)
    table = position[:, None] == jnp.arange(experts * capacity, dtype=jnp.int32)
    return (weights, gate, table)


def dense_chunks(rows, chunks):
    return rows.reshape(chunks, -1, 1024)


def per_device(inputs, routes, router_scores, cotangent, w_gate, w_up, w_down):
    tokens_in = inputs[0]
    upstream = cotangent[0]
    route_col = routes[0][:, 0]
    score_rows = router_scores[0]
    gate_mat = w_gate[0, 0]
    up_mat = w_up[0, 0]
    down_mat = w_down[0, 0]
    experts = lax.axis_size("expert")
    groups = lax.axis_size("dp")
    my_expert = lax.axis_index("expert")
    my_group = lax.axis_index("dp")
    token_count, model_width = tokens_in.shape
    capacity = max(2, token_count * 5 // (4 * experts))
    weights, gate, table = route_tables(route_col, score_rows, experts, capacity)
    table_half = table.astype(jnp.bfloat16)
    token_contract = (((0,), (0,)), ((), ()))
    feature_contract = (((1,), (1,)), ((), ()))
    scaled = (gate[:, None] * upstream.astype(jnp.float32)).astype(jnp.bfloat16)
    local_x = lax.dot_general(
        table_half, tokens_in, token_contract, preferred_element_type=jnp.float32
    ).astype(jnp.bfloat16)
    local_dy = lax.dot_general(
        table_half, scaled, token_contract, preferred_element_type=jnp.float32
    ).astype(jnp.bfloat16)
    pieces = 1
    width = model_width // pieces
    rows_x = []
    rows_grad = []
    for q in range(pieces):
        cols = slice(q * width, (q + 1) * width)
        x_e = lax.all_to_all(dense_chunks(local_x[:, cols], experts), "expert", 0, 0, tiled=True)
        x_e = x_e.reshape(experts * capacity, width)
        rows_x.append(ring_gather(x_e, "dp", my_group))
    for q in range(pieces):
        cols = slice(q * width, (q + 1) * width)
        dy_e = lax.all_to_all(dense_chunks(local_dy[:, cols], experts), "expert", 0, 0, tiled=True)
        dy_e = dy_e.reshape(experts * capacity, width)
        rows_grad.append(ring_gather(dy_e, "dp", my_group))
    gate_pre = 0.0
    up_pre = 0.0
    for q in range(pieces):
        cols = slice(q * width, (q + 1) * width)
        gate_pre = gate_pre + lax.dot_general(
            rows_x[q], gate_mat[:, cols], feature_contract, preferred_element_type=jnp.float32
        )
        up_pre = up_pre + lax.dot_general(
            rows_x[q], up_mat[:, cols], feature_contract, preferred_element_type=jnp.float32
        )
    gate_sig = jax.nn.sigmoid(gate_pre)
    activated = (gate_pre * gate_sig * up_pre).astype(jnp.bfloat16)
    row_score = 0.0
    hidden_grad = 0.0
    for q in range(pieces):
        cols = slice(q * width, (q + 1) * width)
        partial_out = jnp.dot(activated, down_mat[:, cols], preferred_element_type=jnp.float32)
        row_score = row_score + jnp.sum(partial_out * rows_grad[q].astype(jnp.float32), axis=1)
        hidden_grad = hidden_grad + lax.dot_general(
            rows_grad[q], down_mat[:, cols], feature_contract, preferred_element_type=jnp.float32
        )
    pre_gate = (hidden_grad * up_pre * gate_sig * (1.0 + gate_pre * (1.0 - gate_sig))).astype(
        jnp.bfloat16
    )
    pre_up = (hidden_grad * gate_pre * gate_sig).astype(jnp.bfloat16)
    grad_down = []
    grad_gate = []
    grad_up = []
    for q in range(pieces):
        grad_down.append(lax.dot_general(
            activated, rows_grad[q], token_contract, preferred_element_type=jnp.float32
        ).astype(jnp.bfloat16))
        grad_gate.append(lax.dot_general(
            pre_gate, rows_x[q], token_contract, preferred_element_type=jnp.float32
        ).astype(jnp.bfloat16))
        grad_up.append(lax.dot_general(
            pre_up, rows_x[q], token_contract, preferred_element_type=jnp.float32
        ).astype(jnp.bfloat16))
    grad_down = jnp.concatenate(grad_down, axis=1)
    grad_gate = jnp.concatenate(grad_gate, axis=1)
    grad_up = jnp.concatenate(grad_up, axis=1)
    back_pieces = 2
    back_width = model_width // back_pieces
    handed = []
    for q in range(back_pieces):
        cols = slice(q * back_width, (q + 1) * back_width)
        partial_in = jnp.dot(pre_gate, gate_mat[:, cols], preferred_element_type=jnp.float32)
        partial_in = partial_in + jnp.dot(pre_up, up_mat[:, cols], preferred_element_type=jnp.float32)
        if q == 0:
            score_cols = jnp.pad(row_score[:, None], ((0, 0), (0, 127)))
            partial_in = jnp.concatenate([partial_in, score_cols], axis=1)
        summed = ring_reduce_scatter(partial_in.astype(jnp.bfloat16), "dp", my_group)
        span = capacity * back_width // 8
        body = summed[:, :back_width].reshape(experts, 8, span)
        if q == 0:
            tail = summed[:, back_width].reshape(experts, 1, capacity)
            tail = jnp.pad(tail, ((0, 0), (0, 7), (0, 128 - capacity)))
            body = jnp.concatenate([body, tail], axis=2)
        back = lax.all_to_all(body, "expert", 0, 0, tiled=True)
        if q == 0:
            slot_score = back[:, 0, span : span + capacity]
        flat_in = back[:, :, :span].reshape(experts * capacity, back_width)
        piece_grad = jnp.dot(table_half, flat_in, preferred_element_type=jnp.float32).astype(
            jnp.bfloat16
        )
        handed.append(from_behind(piece_grad, "pipe", -1))
    handed = jnp.concatenate(handed, axis=1)
    slot_score = slot_score.astype(jnp.float32).reshape(-1)
    picked = jnp.sum(jnp.where(table, slot_score[None, :], jnp.float32(0.0)), axis=1)
    gate_grad = picked / gate
    is_first = (jnp.arange(score_rows.shape[1]) == 0).astype(jnp.float32)
    score_grad = gate_grad[:, None] * weights[:, 0:1] * (is_first - weights)
    return (
        score_grad[None],
        handed[None],
        grad_gate[None, None],
        grad_up[None, None],
        grad_down[None, None],
    )


def solution(mesh):
    in_specs = (
        P("pipe", ("expert", "dp"), None),
        P("pipe", ("expert", "dp"), None),
        P("pipe", ("expert", "dp"), None),
        P("pipe", ("expert", "dp"), None),
        P("pipe", "expert", "dp", None),
        P("pipe", "expert", "dp", None),
        P("pipe", "expert", "dp", None),
    )
    out_specs = (
        P("pipe", ("expert", "dp"), None),
        P("pipe", ("expert", "dp"), None),
        P("pipe", "expert", "dp", None),
        P("pipe", "expert", "dp", None),
        P("pipe", "expert", "dp", None),
    )
    return jax.shard_map(
        per_device, mesh=mesh, in_specs=in_specs, out_specs=out_specs, check_vma=False
    )
```

```python
import jax
import jax.numpy as jnp
from jax import lax
from jax.sharding import PartitionSpec as P


def from_behind(shard, axis, by):
    length = lax.axis_size(axis)
    pairs = [(i, i + by) for i in range(length) if 0 <= i + by < length]
    return lax.ppermute(shard, axis, pairs)


def ring_gather(piece, axis, me):
    size = lax.axis_size(axis)
    rows = piece.shape[0]
    half = rows // 2
    fwd = [(k, (k + 1) % size) for k in range(size)]
    bwd = [(k, (k - 1) % size) for k in range(size)]
    from_left = lax.ppermute(piece, axis, fwd)
    from_right = lax.ppermute(piece, axis, bwd)
    far_top = lax.ppermute(from_left[:half], axis, fwd)
    far_bottom = lax.ppermute(from_right[half:], axis, bwd)
    whole = jnp.zeros((size * rows,) + piece.shape[1:], piece.dtype)
    whole = lax.dynamic_update_slice_in_dim(whole, piece, me * rows, 0)
    whole = lax.dynamic_update_slice_in_dim(whole, from_left, ((me - 1) % size) * rows, 0)
    whole = lax.dynamic_update_slice_in_dim(whole, from_right, ((me + 1) % size) * rows, 0)
    far = jnp.concatenate([far_top, far_bottom], axis=0)
    whole = lax.dynamic_update_slice_in_dim(whole, far, ((me + 2) % size) * rows, 0)
    return whole


def ring_reduce_scatter(parts, axis, me):
    size = lax.axis_size(axis)
    rows = parts.shape[0] // size
    half = rows // 2
    fwd = [(k, (k + 1) % size) for k in range(size)]
    bwd = [(k, (k - 1) % size) for k in range(size)]

    def block(t):
        return lax.dynamic_slice_in_dim(parts, (t % size) * rows, rows, 0)

    far = block(me + 2)
    got_top = lax.ppermute(far[:half], axis, fwd)
    got_bottom = lax.ppermute(far[half:], axis, bwd)
    to_right = block(me + 1).astype(jnp.float32)
    to_right = jnp.concatenate([to_right[:half] + got_top.astype(jnp.float32), to_right[half:]])
    to_left = block(me - 1).astype(jnp.float32)
    to_left = jnp.concatenate([to_left[:half], to_left[half:] + got_bottom.astype(jnp.float32)])
    from_left = lax.ppermute(to_right.astype(jnp.bfloat16), axis, fwd)
    from_right = lax.ppermute(to_left.astype(jnp.bfloat16), axis, bwd)
    total = block(me).astype(jnp.float32) + from_left.astype(jnp.float32)
    total = total + from_right.astype(jnp.float32)
    return total.astype(jnp.bfloat16)


def route_tables(route_col, score_rows, experts, capacity):
    expert_ids = jnp.arange(experts, dtype=jnp.int32)
    onehot = (route_col[:, None] == expert_ids).astype(jnp.int32)
    earlier = jnp.cumsum(onehot, axis=0) - onehot
    slot = jnp.sum(onehot * earlier, axis=1)
    position = route_col * capacity + slot
    raised = jnp.exp(score_rows)
    weights = raised / jnp.sum(raised, axis=1, keepdims=True)
    gate = lax.optimization_barrier(weights[:, 0].astype(jnp.bfloat16)).astype(jnp.float32)
    table = position[:, None] == jnp.arange(experts * capacity, dtype=jnp.int32)
    return (weights, gate, table)


def dense_chunks(rows, chunks):
    return rows.reshape(chunks, 8, -1)


def per_device(inputs, routes, router_scores, cotangent, w_gate, w_up, w_down):
    tokens_in = inputs[0]
    upstream = cotangent[0]
    route_col = routes[0][:, 0]
    score_rows = router_scores[0]
    gate_mat = w_gate[0, 0]
    up_mat = w_up[0, 0]
    down_mat = w_down[0, 0]
    experts = lax.axis_size("expert")
    groups = lax.axis_size("dp")
    my_expert = lax.axis_index("expert")
    my_group = lax.axis_index("dp")
    token_count, model_width = tokens_in.shape
    capacity = max(2, token_count * 5 // (4 * experts))
    weights, gate, table = route_tables(route_col, score_rows, experts, capacity)
    table_half = table.astype(jnp.bfloat16)
    token_contract = (((0,), (0,)), ((), ()))
    feature_contract = (((1,), (1,)), ((), ()))
    scaled = (gate[:, None] * upstream.astype(jnp.float32)).astype(jnp.bfloat16)
    local_x = lax.dot_general(
        table_half, tokens_in, token_contract, preferred_element_type=jnp.float32
    ).astype(jnp.bfloat16)
    local_dy = lax.dot_general(
        table_half, scaled, token_contract, preferred_element_type=jnp.float32
    ).astype(jnp.bfloat16)
    pieces = 2
    width = model_width // pieces
    rows_x = []
    rows_grad = []
    for q in range(pieces):
        cols = slice(q * width, (q + 1) * width)
        x_e = lax.all_to_all(dense_chunks(local_x[:, cols], experts), "expert", 0, 0, tiled=True)
        x_e = x_e.reshape(experts * capacity, width)
        rows_x.append(ring_gather(x_e, "dp", my_group))
    for q in range(pieces):
        cols = slice(q * width, (q + 1) * width)
        dy_e = lax.all_to_all(dense_chunks(local_dy[:, cols], experts), "expert", 0, 0, tiled=True)
        dy_e = dy_e.reshape(experts * capacity, width)
        rows_grad.append(ring_gather(dy_e, "dp", my_group))
    gate_pre = 0.0
    up_pre = 0.0
    for q in range(pieces):
        cols = slice(q * width, (q + 1) * width)
        gate_pre = gate_pre + lax.dot_general(
            rows_x[q], gate_mat[:, cols], feature_contract, preferred_element_type=jnp.float32
        )
        up_pre = up_pre + lax.dot_general(
            rows_x[q], up_mat[:, cols], feature_contract, preferred_element_type=jnp.float32
        )
    gate_sig = jax.nn.sigmoid(gate_pre)
    activated = (gate_pre * gate_sig * up_pre).astype(jnp.bfloat16)
    row_score = 0.0
    hidden_grad = 0.0
    for q in range(pieces):
        cols = slice(q * width, (q + 1) * width)
        partial_out = jnp.dot(activated, down_mat[:, cols], preferred_element_type=jnp.float32)
        row_score = row_score + jnp.sum(partial_out * rows_grad[q].astype(jnp.float32), axis=1)
        hidden_grad = hidden_grad + lax.dot_general(
            rows_grad[q], down_mat[:, cols], feature_contract, preferred_element_type=jnp.float32
        )
    pre_gate = (hidden_grad * up_pre * gate_sig * (1.0 + gate_pre * (1.0 - gate_sig))).astype(
        jnp.bfloat16
    )
    pre_up = (hidden_grad * gate_pre * gate_sig).astype(jnp.bfloat16)
    grad_down = []
    grad_gate = []
    grad_up = []
    for q in range(pieces):
        grad_down.append(lax.dot_general(
            activated, rows_grad[q], token_contract, preferred_element_type=jnp.float32
        ).astype(jnp.bfloat16))
        grad_gate.append(lax.dot_general(
            pre_gate, rows_x[q], token_contract, preferred_element_type=jnp.float32
        ).astype(jnp.bfloat16))
        grad_up.append(lax.dot_general(
            pre_up, rows_x[q], token_contract, preferred_element_type=jnp.float32
        ).astype(jnp.bfloat16))
    grad_down = jnp.concatenate(grad_down, axis=1)
    grad_gate = jnp.concatenate(grad_gate, axis=1)
    grad_up = jnp.concatenate(grad_up, axis=1)
    back_pieces = 2
    back_width = model_width // back_pieces
    handed = []
    for q in range(back_pieces):
        cols = slice(q * back_width, (q + 1) * back_width)
        partial_in = jnp.dot(pre_gate, gate_mat[:, cols], preferred_element_type=jnp.float32)
        partial_in = partial_in + jnp.dot(pre_up, up_mat[:, cols], preferred_element_type=jnp.float32)
        if q == 0:
            score_cols = jnp.pad(row_score[:, None], ((0, 0), (0, 127)))
            partial_in = jnp.concatenate([partial_in, score_cols], axis=1)
        summed = ring_reduce_scatter(partial_in.astype(jnp.bfloat16), "dp", my_group)
        span = capacity * back_width // 8
        body = summed[:, :back_width].reshape(experts, 8, span)
        if q == 0:
            tail = summed[:, back_width].reshape(experts, 1, capacity)
            tail = jnp.pad(tail, ((0, 0), (0, 7), (0, 128 - capacity)))
            body = jnp.concatenate([body, tail], axis=2)
        back = lax.all_to_all(body, "expert", 0, 0, tiled=True)
        if q == 0:
            slot_score = back[:, 0, span : span + capacity]
        flat_in = back[:, :, :span].reshape(experts * capacity, back_width)
        piece_grad = jnp.dot(table_half, flat_in, preferred_element_type=jnp.float32).astype(
            jnp.bfloat16
        )
        handed.append(from_behind(piece_grad, "pipe", -1))
    handed = jnp.concatenate(handed, axis=1)
    slot_score = slot_score.astype(jnp.float32).reshape(-1)
    picked = jnp.sum(jnp.where(table, slot_score[None, :], jnp.float32(0.0)), axis=1)
    gate_grad = picked / gate
    is_first = (jnp.arange(score_rows.shape[1]) == 0).astype(jnp.float32)
    score_grad = gate_grad[:, None] * weights[:, 0:1] * (is_first - weights)
    return (
        score_grad[None],
        handed[None],
        grad_gate[None, None],
        grad_up[None, None],
        grad_down[None, None],
    )


def solution(mesh):
    in_specs = (
        P("pipe", ("expert", "dp"), None),
        P("pipe", ("expert", "dp"), None),
        P("pipe", ("expert", "dp"), None),
        P("pipe", ("expert", "dp"), None),
        P("pipe", "expert", "dp", None),
        P("pipe", "expert", "dp", None),
        P("pipe", "expert", "dp", None),
    )
    out_specs = (
        P("pipe", ("expert", "dp"), None),
        P("pipe", ("expert", "dp"), None),
        P("pipe", "expert", "dp", None),
        P("pipe", "expert", "dp", None),
        P("pipe", "expert", "dp", None),
    )
    return jax.shard_map(
        per_device, mesh=mesh, in_specs=in_specs, out_specs=out_specs, check_vma=False
    )
```

```python
import jax
import jax.numpy as jnp
from jax import lax
from jax.sharding import PartitionSpec as P


def from_behind(shard, axis, by):
    length = lax.axis_size(axis)
    pairs = [(i, i + by) for i in range(length) if 0 <= i + by < length]
    return lax.ppermute(shard, axis, pairs)


def ring_gather(piece, axis, me):
    size = lax.axis_size(axis)
    rows = piece.shape[0]
    half = rows // 2
    fwd = [(k, (k + 1) % size) for k in range(size)]
    bwd = [(k, (k - 1) % size) for k in range(size)]
    from_left = lax.ppermute(piece, axis, fwd)
    from_right = lax.ppermute(piece, axis, bwd)
    far_top = lax.ppermute(from_left[:half], axis, fwd)
    far_bottom = lax.ppermute(from_right[half:], axis, bwd)
    far = jnp.concatenate([far_top, far_bottom], axis=0)
    return jnp.concatenate([piece, from_right, far, from_left], axis=0)


def ring_reduce_scatter(parts, axis, me):
    size = lax.axis_size(axis)
    rows = parts.shape[0] // size
    half = rows // 2
    fwd = [(k, (k + 1) % size) for k in range(size)]
    bwd = [(k, (k - 1) % size) for k in range(size)]

    def block(offset):
        return parts[offset * rows : (offset + 1) * rows]

    far = block(2)
    got_top = lax.ppermute(far[:half], axis, fwd)
    got_bottom = lax.ppermute(far[half:], axis, bwd)
    to_right = block(1).astype(jnp.float32)
    to_right = jnp.concatenate([to_right[:half] + got_top.astype(jnp.float32), to_right[half:]])
    to_left = block(size - 1).astype(jnp.float32)
    to_left = jnp.concatenate([to_left[:half], to_left[half:] + got_bottom.astype(jnp.float32)])
    from_left = lax.ppermute(to_right.astype(jnp.bfloat16), axis, fwd)
    from_right = lax.ppermute(to_left.astype(jnp.bfloat16), axis, bwd)
    total = block(0).astype(jnp.float32) + from_left.astype(jnp.float32)
    total = total + from_right.astype(jnp.float32)
    return total.astype(jnp.bfloat16)


def route_tables(route_col, score_rows, experts, capacity):
    expert_ids = jnp.arange(experts, dtype=jnp.int32)
    onehot = (route_col[:, None] == expert_ids).astype(jnp.int32)
    earlier = jnp.cumsum(onehot, axis=0) - onehot
    slot = jnp.sum(onehot * earlier, axis=1)
    position = route_col * capacity + slot
    raised = jnp.exp(score_rows)
    weights = raised / jnp.sum(raised, axis=1, keepdims=True)
    gate = lax.optimization_barrier(weights[:, 0].astype(jnp.bfloat16)).astype(jnp.float32)
    table = position[:, None] == jnp.arange(experts * capacity, dtype=jnp.int32)
    return (weights, gate, table)


def dense_chunks(rows, chunks):
    return rows.reshape(chunks, -1, 1024)


def per_device(inputs, routes, router_scores, cotangent, w_gate, w_up, w_down):
    tokens_in = inputs[0]
    upstream = cotangent[0]
    route_col = routes[0][:, 0]
    score_rows = router_scores[0]
    gate_mat = w_gate[0, 0]
    up_mat = w_up[0, 0]
    down_mat = w_down[0, 0]
    experts = lax.axis_size("expert")
    groups = lax.axis_size("dp")
    my_expert = lax.axis_index("expert")
    my_group = lax.axis_index("dp")
    token_count, model_width = tokens_in.shape
    capacity = max(2, token_count * 5 // (4 * experts))
    weights, gate, table = route_tables(route_col, score_rows, experts, capacity)
    table_half = table.astype(jnp.bfloat16)
    token_contract = (((0,), (0,)), ((), ()))
    feature_contract = (((1,), (1,)), ((), ()))
    scaled = (gate[:, None] * upstream.astype(jnp.float32)).astype(jnp.bfloat16)
    local_x = lax.dot_general(
        table_half, tokens_in, token_contract, preferred_element_type=jnp.float32
    ).astype(jnp.bfloat16)
    local_dy = lax.dot_general(
        table_half, scaled, token_contract, preferred_element_type=jnp.float32
    ).astype(jnp.bfloat16)
    pieces = 1
    width = model_width // pieces
    rows_x = []
    rows_grad = []
    for q in range(pieces):
        cols = slice(q * width, (q + 1) * width)
        x_e = lax.all_to_all(dense_chunks(local_x[:, cols], experts), "expert", 0, 0, tiled=True)
        x_e = x_e.reshape(experts * capacity, width)
        rows_x.append(ring_gather(x_e, "dp", my_group))
    for q in range(pieces):
        cols = slice(q * width, (q + 1) * width)
        dy_e = lax.all_to_all(dense_chunks(local_dy[:, cols], experts), "expert", 0, 0, tiled=True)
        dy_e = dy_e.reshape(experts * capacity, width)
        rows_grad.append(ring_gather(dy_e, "dp", my_group))
    both_mat = jnp.concatenate([gate_mat, up_mat], axis=0)
    hidden = gate_mat.shape[0]
    both_pre = 0.0
    for q in range(pieces):
        cols = slice(q * width, (q + 1) * width)
        both_pre = both_pre + lax.dot_general(
            rows_x[q], both_mat[:, cols], feature_contract, preferred_element_type=jnp.float32
        )
    gate_pre = both_pre[:, :hidden]
    up_pre = both_pre[:, hidden:]
    gate_sig = jax.nn.sigmoid(gate_pre)
    activated = (gate_pre * gate_sig * up_pre).astype(jnp.bfloat16)
    row_score = 0.0
    hidden_grad = 0.0
    for q in range(pieces):
        cols = slice(q * width, (q + 1) * width)
        partial_out = jnp.dot(activated, down_mat[:, cols], preferred_element_type=jnp.float32)
        row_score = row_score + jnp.sum(partial_out * rows_grad[q].astype(jnp.float32), axis=1)
        hidden_grad = hidden_grad + lax.dot_general(
            rows_grad[q], down_mat[:, cols], feature_contract, preferred_element_type=jnp.float32
        )
    pre_gate = (hidden_grad * up_pre * gate_sig * (1.0 + gate_pre * (1.0 - gate_sig))).astype(
        jnp.bfloat16
    )
    pre_up = (hidden_grad * gate_pre * gate_sig).astype(jnp.bfloat16)
    pre_both = jnp.concatenate([pre_gate, pre_up], axis=1)
    grad_down = []
    grad_gate = []
    grad_up = []
    for q in range(pieces):
        grad_down.append(lax.dot_general(
            activated, rows_grad[q], token_contract, preferred_element_type=jnp.float32
        ).astype(jnp.bfloat16))
        grad_both = lax.dot_general(
            pre_both, rows_x[q], token_contract, preferred_element_type=jnp.float32
        ).astype(jnp.bfloat16)
        grad_gate.append(grad_both[:hidden])
        grad_up.append(grad_both[hidden:])
    grad_down = jnp.concatenate(grad_down, axis=1)
    grad_gate = jnp.concatenate(grad_gate, axis=1)
    grad_up = jnp.concatenate(grad_up, axis=1)
    back_pieces = 2
    back_width = model_width // back_pieces
    handed = []
    for q in range(back_pieces):
        cols = slice(q * back_width, (q + 1) * back_width)
        partial_in = jnp.dot(pre_both, both_mat[:, cols], preferred_element_type=jnp.float32)
        if q == 0:
            score_cols = jnp.pad(row_score[:, None], ((0, 0), (0, 127)))
            partial_in = jnp.concatenate([partial_in, score_cols], axis=1)
        summed = ring_reduce_scatter(partial_in.astype(jnp.bfloat16), "dp", my_group)
        span = capacity * back_width // 8
        body = summed[:, :back_width].reshape(experts, 8, span)
        if q == 0:
            tail = summed[:, back_width].reshape(experts, 1, capacity)
            tail = jnp.pad(tail, ((0, 0), (0, 7), (0, 128 - capacity)))
            body = jnp.concatenate([body, tail], axis=2)
        back = lax.all_to_all(body, "expert", 0, 0, tiled=True)
        if q == 0:
            slot_score = back[:, 0, span : span + capacity]
        flat_in = back[:, :, :span].reshape(experts * capacity, back_width)
        piece_grad = jnp.dot(table_half, flat_in, preferred_element_type=jnp.float32).astype(
            jnp.bfloat16
        )
        handed.append(from_behind(piece_grad, "pipe", -1))
    handed = jnp.concatenate(handed, axis=1)
    slot_score = slot_score.astype(jnp.float32).reshape(-1)
    picked = jnp.sum(jnp.where(table, slot_score[None, :], jnp.float32(0.0)), axis=1)
    gate_grad = picked / gate
    is_first = (jnp.arange(score_rows.shape[1]) == 0).astype(jnp.float32)
    score_grad = gate_grad[:, None] * weights[:, 0:1] * (is_first - weights)
    return (
        score_grad[None],
        handed[None],
        grad_gate[None, None],
        grad_up[None, None],
        grad_down[None, None],
    )


def solution(mesh):
    in_specs = (
        P("pipe", ("expert", "dp"), None),
        P("pipe", ("expert", "dp"), None),
        P("pipe", ("expert", "dp"), None),
        P("pipe", ("expert", "dp"), None),
        P("pipe", "expert", "dp", None),
        P("pipe", "expert", "dp", None),
        P("pipe", "expert", "dp", None),
    )
    out_specs = (
        P("pipe", ("expert", "dp"), None),
        P("pipe", ("expert", "dp"), None),
        P("pipe", "expert", "dp", None),
        P("pipe", "expert", "dp", None),
        P("pipe", "expert", "dp", None),
    )
    return jax.shard_map(
        per_device, mesh=mesh, in_specs=in_specs, out_specs=out_specs, check_vma=False
    )
```

```python
import jax
import jax.numpy as jnp
from jax import lax
from jax.sharding import PartitionSpec as P


def from_behind(shard, axis, by):
    length = lax.axis_size(axis)
    pairs = [(i, i + by) for i in range(length) if 0 <= i + by < length]
    return lax.ppermute(shard, axis, pairs)


def ring_gather(piece, axis, me):
    size = lax.axis_size(axis)
    rows = piece.shape[0]
    half = rows // 2
    fwd = [(k, (k + 1) % size) for k in range(size)]
    bwd = [(k, (k - 1) % size) for k in range(size)]
    from_left = lax.ppermute(piece, axis, fwd)
    from_right = lax.ppermute(piece, axis, bwd)
    far_top = lax.ppermute(from_left[:half], axis, fwd)
    far_bottom = lax.ppermute(from_right[half:], axis, bwd)
    far = jnp.concatenate([far_top, far_bottom], axis=0)
    return jnp.concatenate([piece, from_right, far, from_left], axis=0)


def ring_reduce_scatter(parts, axis, me):
    size = lax.axis_size(axis)
    rows = parts.shape[0] // size
    half = rows // 2
    fwd = [(k, (k + 1) % size) for k in range(size)]
    bwd = [(k, (k - 1) % size) for k in range(size)]

    def block(offset):
        return parts[offset * rows : (offset + 1) * rows]

    far = block(2)
    got_top = lax.ppermute(far[:half], axis, fwd)
    got_bottom = lax.ppermute(far[half:], axis, bwd)
    to_right = block(1).astype(jnp.float32)
    to_right = jnp.concatenate([to_right[:half] + got_top.astype(jnp.float32), to_right[half:]])
    to_left = block(size - 1).astype(jnp.float32)
    to_left = jnp.concatenate([to_left[:half], to_left[half:] + got_bottom.astype(jnp.float32)])
    from_left = lax.ppermute(to_right.astype(jnp.bfloat16), axis, fwd)
    from_right = lax.ppermute(to_left.astype(jnp.bfloat16), axis, bwd)
    total = block(0).astype(jnp.float32) + from_left.astype(jnp.float32)
    total = total + from_right.astype(jnp.float32)
    return total.astype(jnp.bfloat16)


def route_tables(route_col, score_rows, experts, capacity):
    expert_ids = jnp.arange(experts, dtype=jnp.int32)
    onehot = (route_col[:, None] == expert_ids).astype(jnp.int32)
    earlier = jnp.cumsum(onehot, axis=0) - onehot
    slot = jnp.sum(onehot * earlier, axis=1)
    position = route_col * capacity + slot
    raised = jnp.exp(score_rows)
    weights = raised / jnp.sum(raised, axis=1, keepdims=True)
    gate = lax.optimization_barrier(weights[:, 0].astype(jnp.bfloat16)).astype(jnp.float32)
    table = position[:, None] == jnp.arange(experts * capacity, dtype=jnp.int32)
    return (weights, gate, table)


def dense_chunks(rows, chunks):
    return rows.reshape(chunks, -1, 1024)


def per_device(inputs, routes, router_scores, cotangent, w_gate, w_up, w_down):
    tokens_in = inputs[0]
    upstream = cotangent[0]
    route_col = routes[0][:, 0]
    score_rows = router_scores[0]
    gate_mat = w_gate[0, 0]
    up_mat = w_up[0, 0]
    down_mat = w_down[0, 0]
    experts = lax.axis_size("expert")
    groups = lax.axis_size("dp")
    my_expert = lax.axis_index("expert")
    my_group = lax.axis_index("dp")
    token_count, model_width = tokens_in.shape
    capacity = max(2, token_count * 5 // (4 * experts))
    weights, gate, table = route_tables(route_col, score_rows, experts, capacity)
    table_half = table.astype(jnp.bfloat16)
    token_contract = (((0,), (0,)), ((), ()))
    feature_contract = (((1,), (1,)), ((), ()))
    scaled = (gate[:, None] * upstream.astype(jnp.float32)).astype(jnp.bfloat16)
    local_x = lax.dot_general(
        table_half, tokens_in, token_contract, preferred_element_type=jnp.float32
    ).astype(jnp.bfloat16)
    local_dy = lax.dot_general(
        table_half, scaled, token_contract, preferred_element_type=jnp.float32
    ).astype(jnp.bfloat16)
    pieces = 1
    width = model_width // pieces
    rows_x = []
    rows_grad = []
    for q in range(pieces):
        cols = slice(q * width, (q + 1) * width)
        x_e = lax.all_to_all(dense_chunks(local_x[:, cols], experts), "expert", 0, 0, tiled=True)
        x_e = x_e.reshape(experts * capacity, width)
        rows_x.append(ring_gather(x_e, "dp", my_group))
    for q in range(pieces):
        cols = slice(q * width, (q + 1) * width)
        dy_e = lax.all_to_all(dense_chunks(local_dy[:, cols], experts), "expert", 0, 0, tiled=True)
        dy_e = dy_e.reshape(experts * capacity, width)
        rows_grad.append(ring_gather(dy_e, "dp", my_group))
    both_mat = jnp.concatenate([gate_mat, up_mat], axis=0)
    hidden = gate_mat.shape[0]
    both_pre = 0.0
    for q in range(pieces):
        cols = slice(q * width, (q + 1) * width)
        both_pre = both_pre + lax.dot_general(
            rows_x[q], both_mat[:, cols], feature_contract, preferred_element_type=jnp.float32
        )
    gate_pre = both_pre[:, :hidden]
    up_pre = both_pre[:, hidden:]
    gate_sig = jax.nn.sigmoid(gate_pre)
    activated = (gate_pre * gate_sig * up_pre).astype(jnp.bfloat16)
    row_score = 0.0
    hidden_grad = 0.0
    for q in range(pieces):
        cols = slice(q * width, (q + 1) * width)
        partial_out = jnp.dot(activated, down_mat[:, cols], preferred_element_type=jnp.float32)
        row_score = row_score + jnp.sum(partial_out * rows_grad[q].astype(jnp.float32), axis=1)
        hidden_grad = hidden_grad + lax.dot_general(
            rows_grad[q], down_mat[:, cols], feature_contract, preferred_element_type=jnp.float32
        )
    pre_gate = (hidden_grad * up_pre * gate_sig * (1.0 + gate_pre * (1.0 - gate_sig))).astype(
        jnp.bfloat16
    )
    pre_up = (hidden_grad * gate_pre * gate_sig).astype(jnp.bfloat16)
    pre_both = jnp.concatenate([pre_gate, pre_up], axis=1)
    grad_down = []
    grad_gate = []
    grad_up = []
    for q in range(pieces):
        grad_down.append(lax.dot_general(
            activated, rows_grad[q], token_contract, preferred_element_type=jnp.float32
        ).astype(jnp.bfloat16))
        grad_both = lax.dot_general(
            pre_both, rows_x[q], token_contract, preferred_element_type=jnp.float32
        ).astype(jnp.bfloat16)
        grad_gate.append(grad_both[:hidden])
        grad_up.append(grad_both[hidden:])
    grad_down = jnp.concatenate(grad_down, axis=1)
    grad_gate = jnp.concatenate(grad_gate, axis=1)
    grad_up = jnp.concatenate(grad_up, axis=1)
    unit = model_width // 8
    back_widths = [4 * unit, 3 * unit, unit]
    handed = []
    offset = 0
    for q, back_width in enumerate(back_widths):
        cols = slice(offset, offset + back_width)
        offset += back_width
        partial_in = jnp.dot(pre_both, both_mat[:, cols], preferred_element_type=jnp.float32)
        if q == 0:
            score_cols = jnp.pad(row_score[:, None], ((0, 0), (0, 127)))
            partial_in = jnp.concatenate([partial_in, score_cols], axis=1)
        summed = ring_reduce_scatter(partial_in.astype(jnp.bfloat16), "dp", my_group)
        span = capacity * back_width // 8
        body = summed[:, :back_width].reshape(experts, 8, span)
        if q == 0:
            tail = summed[:, back_width].reshape(experts, 1, capacity)
            tail = jnp.pad(tail, ((0, 0), (0, 7), (0, 128 - capacity)))
            body = jnp.concatenate([body, tail], axis=2)
        back = lax.all_to_all(body, "expert", 0, 0, tiled=True)
        if q == 0:
            slot_score = back[:, 0, span : span + capacity]
        flat_in = back[:, :, :span].reshape(experts * capacity, back_width)
        piece_grad = jnp.dot(table_half, flat_in, preferred_element_type=jnp.float32).astype(
            jnp.bfloat16
        )
        handed.append(from_behind(piece_grad, "pipe", -1))
    handed = jnp.concatenate(handed, axis=1)
    slot_score = slot_score.astype(jnp.float32).reshape(-1)
    picked = jnp.sum(jnp.where(table, slot_score[None, :], jnp.float32(0.0)), axis=1)
    gate_grad = picked / gate
    is_first = (jnp.arange(score_rows.shape[1]) == 0).astype(jnp.float32)
    score_grad = gate_grad[:, None] * weights[:, 0:1] * (is_first - weights)
    return (
        score_grad[None],
        handed[None],
        grad_gate[None, None],
        grad_up[None, None],
        grad_down[None, None],
    )


def solution(mesh):
    in_specs = (
        P("pipe", ("expert", "dp"), None),
        P("pipe", ("expert", "dp"), None),
        P("pipe", ("expert", "dp"), None),
        P("pipe", ("expert", "dp"), None),
        P("pipe", "expert", "dp", None),
        P("pipe", "expert", "dp", None),
        P("pipe", "expert", "dp", None),
    )
    out_specs = (
        P("pipe", ("expert", "dp"), None),
        P("pipe", ("expert", "dp"), None),
        P("pipe", "expert", "dp", None),
        P("pipe", "expert", "dp", None),
        P("pipe", "expert", "dp", None),
    )
    return jax.shard_map(
        per_device, mesh=mesh, in_specs=in_specs, out_specs=out_specs, check_vma=False
    )
```

```python
import jax
import jax.numpy as jnp
from jax import lax
from jax.sharding import PartitionSpec as P


def from_behind(shard, axis, by):
    length = lax.axis_size(axis)
    pairs = [(i, i + by) for i in range(length) if 0 <= i + by < length]
    return lax.ppermute(shard, axis, pairs)


def ring_gather(piece, axis, me):
    size = lax.axis_size(axis)
    rows = piece.shape[0]
    half = rows // 2
    fwd = [(k, (k + 1) % size) for k in range(size)]
    bwd = [(k, (k - 1) % size) for k in range(size)]
    from_left = lax.ppermute(piece, axis, fwd)
    from_right = lax.ppermute(piece, axis, bwd)
    far_top = lax.ppermute(from_left[:half], axis, fwd)
    far_bottom = lax.ppermute(from_right[half:], axis, bwd)
    far = jnp.concatenate([far_top, far_bottom], axis=0)
    return jnp.concatenate([piece, from_right, far, from_left], axis=0)


def ring_reduce_scatter(parts, axis, me):
    size = lax.axis_size(axis)
    rows = parts.shape[0] // size
    half = rows // 2
    fwd = [(k, (k + 1) % size) for k in range(size)]
    bwd = [(k, (k - 1) % size) for k in range(size)]

    def block(offset):
        return parts[offset * rows : (offset + 1) * rows]

    far = block(2)
    got_top = lax.ppermute(far[:half], axis, fwd)
    got_bottom = lax.ppermute(far[half:], axis, bwd)
    to_right = block(1).astype(jnp.float32)
    to_right = jnp.concatenate([to_right[:half] + got_top.astype(jnp.float32), to_right[half:]])
    to_left = block(size - 1).astype(jnp.float32)
    to_left = jnp.concatenate([to_left[:half], to_left[half:] + got_bottom.astype(jnp.float32)])
    from_left = lax.ppermute(to_right.astype(jnp.bfloat16), axis, fwd)
    from_right = lax.ppermute(to_left.astype(jnp.bfloat16), axis, bwd)
    total = block(0).astype(jnp.float32) + from_left.astype(jnp.float32)
    total = total + from_right.astype(jnp.float32)
    return total.astype(jnp.bfloat16)


def slot_table(route_col, experts, capacity):
    expert_ids = jnp.arange(experts, dtype=jnp.int32)
    onehot = (route_col[:, None] == expert_ids).astype(jnp.int32)
    earlier = jnp.cumsum(onehot, axis=0) - onehot
    slot = jnp.sum(onehot * earlier, axis=1)
    position = route_col * capacity + slot
    return position[:, None] == jnp.arange(experts * capacity, dtype=jnp.int32)


def route_tables(route_col, score_rows, experts, capacity):
    expert_ids = jnp.arange(experts, dtype=jnp.int32)
    onehot = (route_col[:, None] == expert_ids).astype(jnp.int32)
    earlier = jnp.cumsum(onehot, axis=0) - onehot
    slot = jnp.sum(onehot * earlier, axis=1)
    position = route_col * capacity + slot
    raised = jnp.exp(score_rows)
    weights = raised / jnp.sum(raised, axis=1, keepdims=True)
    gate = lax.optimization_barrier(weights[:, 0].astype(jnp.bfloat16)).astype(jnp.float32)
    table = position[:, None] == jnp.arange(experts * capacity, dtype=jnp.int32)
    return (weights, gate, table)


def dense_chunks(rows, chunks):
    return rows.reshape(chunks, -1, 1024)


def per_device(inputs, routes, router_scores, cotangent, w_gate, w_up, w_down):
    tokens_in = inputs[0]
    upstream = cotangent[0]
    route_col = routes[0][:, 0]
    score_rows = router_scores[0]
    gate_mat = w_gate[0, 0]
    up_mat = w_up[0, 0]
    down_mat = w_down[0, 0]
    experts = lax.axis_size("expert")
    groups = lax.axis_size("dp")
    my_expert = lax.axis_index("expert")
    my_group = lax.axis_index("dp")
    token_count, model_width = tokens_in.shape
    capacity = max(2, token_count * 5 // (4 * experts))
    weights, gate, table = route_tables(route_col, score_rows, experts, capacity)
    table_half = table.astype(jnp.bfloat16)
    next_route = from_behind(route_col, "pipe", -1)
    next_table = slot_table(next_route, experts, capacity).astype(jnp.bfloat16)
    token_contract = (((0,), (0,)), ((), ()))
    feature_contract = (((1,), (1,)), ((), ()))
    scaled = (gate[:, None] * upstream.astype(jnp.float32)).astype(jnp.bfloat16)
    local_x = lax.dot_general(
        table_half, tokens_in, token_contract, preferred_element_type=jnp.float32
    ).astype(jnp.bfloat16)
    local_dy = lax.dot_general(
        table_half, scaled, token_contract, preferred_element_type=jnp.float32
    ).astype(jnp.bfloat16)
    pieces = 1
    width = model_width // pieces
    rows_x = []
    rows_grad = []
    for q in range(pieces):
        cols = slice(q * width, (q + 1) * width)
        x_e = lax.all_to_all(dense_chunks(local_x[:, cols], experts), "expert", 0, 0, tiled=True)
        x_e = x_e.reshape(experts * capacity, width)
        rows_x.append(ring_gather(x_e, "dp", my_group))
    for q in range(pieces):
        cols = slice(q * width, (q + 1) * width)
        dy_e = lax.all_to_all(dense_chunks(local_dy[:, cols], experts), "expert", 0, 0, tiled=True)
        dy_e = dy_e.reshape(experts * capacity, width)
        rows_grad.append(ring_gather(dy_e, "dp", my_group))
    both_mat = jnp.concatenate([gate_mat, up_mat], axis=0)
    hidden = gate_mat.shape[0]
    both_pre = 0.0
    for q in range(pieces):
        cols = slice(q * width, (q + 1) * width)
        both_pre = both_pre + lax.dot_general(
            rows_x[q], both_mat[:, cols], feature_contract, preferred_element_type=jnp.float32
        )
    gate_pre = both_pre[:, :hidden]
    up_pre = both_pre[:, hidden:]
    gate_sig = jax.nn.sigmoid(gate_pre)
    activated = (gate_pre * gate_sig * up_pre).astype(jnp.bfloat16)
    row_score = 0.0
    hidden_grad = 0.0
    for q in range(pieces):
        cols = slice(q * width, (q + 1) * width)
        partial_out = jnp.dot(activated, down_mat[:, cols], preferred_element_type=jnp.float32)
        row_score = row_score + jnp.sum(partial_out * rows_grad[q].astype(jnp.float32), axis=1)
        hidden_grad = hidden_grad + lax.dot_general(
            rows_grad[q], down_mat[:, cols], feature_contract, preferred_element_type=jnp.float32
        )
    pre_gate = (hidden_grad * up_pre * gate_sig * (1.0 + gate_pre * (1.0 - gate_sig))).astype(
        jnp.bfloat16
    )
    pre_up = (hidden_grad * gate_pre * gate_sig).astype(jnp.bfloat16)
    pre_both = jnp.concatenate([pre_gate, pre_up], axis=1)
    grad_down = []
    grad_gate = []
    grad_up = []
    for q in range(pieces):
        grad_down.append(lax.dot_general(
            activated, rows_grad[q], token_contract, preferred_element_type=jnp.float32
        ).astype(jnp.bfloat16))
        grad_both = lax.dot_general(
            pre_both, rows_x[q], token_contract, preferred_element_type=jnp.float32
        ).astype(jnp.bfloat16)
        grad_gate.append(grad_both[:hidden])
        grad_up.append(grad_both[hidden:])
    grad_down = jnp.concatenate(grad_down, axis=1)
    grad_gate = jnp.concatenate(grad_gate, axis=1)
    grad_up = jnp.concatenate(grad_up, axis=1)
    back_pieces = 2
    back_width = model_width // back_pieces
    handed = []
    for q in range(back_pieces):
        cols = slice(q * back_width, (q + 1) * back_width)
        partial_in = jnp.dot(pre_both, both_mat[:, cols], preferred_element_type=jnp.float32)
        if q == 0:
            score_cols = jnp.pad(row_score[:, None], ((0, 0), (0, 127)))
            partial_in = jnp.concatenate([partial_in, score_cols], axis=1)
        summed = ring_reduce_scatter(partial_in.astype(jnp.bfloat16), "dp", my_group)
        span = capacity * back_width // 8
        body = summed[:, :back_width].reshape(experts, 8, span)
        if q == 0:
            tail = summed[:, back_width].reshape(experts, 1, capacity)
            tail = jnp.pad(tail, ((0, 0), (0, 7), (0, 128 - capacity)))
            body = jnp.concatenate([body, tail], axis=2)
        last = q == back_pieces - 1
        if last:
            body = from_behind(body, "pipe", -1)
        back = lax.all_to_all(body, "expert", 0, 0, tiled=True)
        if q == 0:
            slot_score = back[:, 0, span : span + capacity]
        flat_in = back[:, :, :span].reshape(experts * capacity, back_width)
        piece_grad = jnp.dot(
            next_table if last else table_half, flat_in, preferred_element_type=jnp.float32
        ).astype(jnp.bfloat16)
        handed.append(piece_grad if last else from_behind(piece_grad, "pipe", -1))
    handed = jnp.concatenate(handed, axis=1)
    slot_score = slot_score.astype(jnp.float32).reshape(-1)
    picked = jnp.sum(jnp.where(table, slot_score[None, :], jnp.float32(0.0)), axis=1)
    gate_grad = picked / gate
    is_first = (jnp.arange(score_rows.shape[1]) == 0).astype(jnp.float32)
    score_grad = gate_grad[:, None] * weights[:, 0:1] * (is_first - weights)
    return (
        score_grad[None],
        handed[None],
        grad_gate[None, None],
        grad_up[None, None],
        grad_down[None, None],
    )


def solution(mesh):
    in_specs = (
        P("pipe", ("expert", "dp"), None),
        P("pipe", ("expert", "dp"), None),
        P("pipe", ("expert", "dp"), None),
        P("pipe", ("expert", "dp"), None),
        P("pipe", "expert", "dp", None),
        P("pipe", "expert", "dp", None),
        P("pipe", "expert", "dp", None),
    )
    out_specs = (
        P("pipe", ("expert", "dp"), None),
        P("pipe", ("expert", "dp"), None),
        P("pipe", "expert", "dp", None),
        P("pipe", "expert", "dp", None),
        P("pipe", "expert", "dp", None),
    )
    return jax.shard_map(
        per_device, mesh=mesh, in_specs=in_specs, out_specs=out_specs, check_vma=False
    )
```

```python
import jax
import jax.numpy as jnp
from jax import lax
from jax.sharding import PartitionSpec as P


def from_behind(shard, axis, by):
    length = lax.axis_size(axis)
    pairs = [(i, i + by) for i in range(length) if 0 <= i + by < length]
    return lax.ppermute(shard, axis, pairs)


def ring_gather(piece, axis, me):
    size = lax.axis_size(axis)
    rows = piece.shape[0]
    half = rows // 2
    fwd = [(k, (k + 1) % size) for k in range(size)]
    bwd = [(k, (k - 1) % size) for k in range(size)]
    from_left = lax.ppermute(piece, axis, fwd)
    from_right = lax.ppermute(piece, axis, bwd)
    far_top = lax.ppermute(from_left[:half], axis, fwd)
    far_bottom = lax.ppermute(from_right[half:], axis, bwd)
    far = jnp.concatenate([far_top, far_bottom], axis=0)
    return jnp.concatenate([piece, from_right, far, from_left], axis=0)


def ring_reduce_scatter(parts, axis, me):
    size = lax.axis_size(axis)
    rows = parts.shape[0] // size
    half = rows // 2
    fwd = [(k, (k + 1) % size) for k in range(size)]
    bwd = [(k, (k - 1) % size) for k in range(size)]

    def block(offset):
        return parts[offset * rows : (offset + 1) * rows]

    far = block(2)
    got_top = lax.ppermute(far[:half], axis, fwd)
    got_bottom = lax.ppermute(far[half:], axis, bwd)
    to_right = block(1).astype(jnp.float32)
    to_right = jnp.concatenate([to_right[:half] + got_top.astype(jnp.float32), to_right[half:]])
    to_left = block(size - 1).astype(jnp.float32)
    to_left = jnp.concatenate([to_left[:half], to_left[half:] + got_bottom.astype(jnp.float32)])
    from_left = lax.ppermute(to_right.astype(jnp.bfloat16), axis, fwd)
    from_right = lax.ppermute(to_left.astype(jnp.bfloat16), axis, bwd)
    total = block(0).astype(jnp.float32) + from_left.astype(jnp.float32)
    total = total + from_right.astype(jnp.float32)
    return total.astype(jnp.bfloat16)


def route_tables(route_col, score_rows, experts, capacity):
    expert_ids = jnp.arange(experts, dtype=jnp.int32)
    onehot = (route_col[:, None] == expert_ids).astype(jnp.int32)
    earlier = jnp.cumsum(onehot, axis=0) - onehot
    slot = jnp.sum(onehot * earlier, axis=1)
    position = route_col * capacity + slot
    raised = jnp.exp(score_rows)
    weights = raised / jnp.sum(raised, axis=1, keepdims=True)
    gate = lax.optimization_barrier(weights[:, 0].astype(jnp.bfloat16)).astype(jnp.float32)
    table = position[:, None] == jnp.arange(experts * capacity, dtype=jnp.int32)
    return (weights, gate, table)


def dense_chunks(rows, chunks):
    return rows.reshape(chunks, -1, 1024)


def per_device(inputs, routes, router_scores, cotangent, w_gate, w_up, w_down):
    tokens_in = inputs[0]
    upstream = cotangent[0]
    route_col = routes[0][:, 0]
    score_rows = router_scores[0]
    gate_mat = w_gate[0, 0]
    up_mat = w_up[0, 0]
    down_mat = w_down[0, 0]
    experts = lax.axis_size("expert")
    groups = lax.axis_size("dp")
    my_expert = lax.axis_index("expert")
    my_group = lax.axis_index("dp")
    token_count, model_width = tokens_in.shape
    capacity = max(2, token_count * 5 // (4 * experts))
    weights, gate, table = route_tables(route_col, score_rows, experts, capacity)
    table_half = table.astype(jnp.bfloat16)
    token_contract = (((0,), (0,)), ((), ()))
    feature_contract = (((1,), (1,)), ((), ()))
    scaled = (gate[:, None] * upstream.astype(jnp.float32)).astype(jnp.bfloat16)
    local_x = lax.dot_general(
        table_half, tokens_in, token_contract, preferred_element_type=jnp.float32
    ).astype(jnp.bfloat16)
    local_dy = lax.dot_general(
        table_half, scaled, token_contract, preferred_element_type=jnp.float32
    ).astype(jnp.bfloat16)
    pieces = 1
    width = model_width // pieces
    rows_x = []
    rows_grad = []
    for q in range(pieces):
        cols = slice(q * width, (q + 1) * width)
        x_e = lax.all_to_all(dense_chunks(local_x[:, cols], experts), "expert", 0, 0, tiled=True)
        x_e = x_e.reshape(experts * capacity, width)
        rows_x.append(ring_gather(x_e, "dp", my_group))
    for q in range(pieces):
        cols = slice(q * width, (q + 1) * width)
        dy_e = lax.all_to_all(dense_chunks(local_dy[:, cols], experts), "expert", 0, 0, tiled=True)
        dy_e = dy_e.reshape(experts * capacity, width)
        dy_e, rows_x[q] = lax.optimization_barrier((dy_e, rows_x[q]))
        rows_grad.append(ring_gather(dy_e, "dp", my_group))
    both_mat = jnp.concatenate([gate_mat, up_mat], axis=0)
    hidden = gate_mat.shape[0]
    both_pre = 0.0
    for q in range(pieces):
        cols = slice(q * width, (q + 1) * width)
        both_pre = both_pre + lax.dot_general(
            rows_x[q], both_mat[:, cols], feature_contract, preferred_element_type=jnp.float32
        )
    gate_pre = both_pre[:, :hidden]
    up_pre = both_pre[:, hidden:]
    gate_sig = jax.nn.sigmoid(gate_pre)
    activated = (gate_pre * gate_sig * up_pre).astype(jnp.bfloat16)
    row_score = 0.0
    hidden_grad = 0.0
    for q in range(pieces):
        cols = slice(q * width, (q + 1) * width)
        partial_out = jnp.dot(activated, down_mat[:, cols], preferred_element_type=jnp.float32)
        row_score = row_score + jnp.sum(partial_out * rows_grad[q].astype(jnp.float32), axis=1)
        hidden_grad = hidden_grad + lax.dot_general(
            rows_grad[q], down_mat[:, cols], feature_contract, preferred_element_type=jnp.float32
        )
    pre_gate = (hidden_grad * up_pre * gate_sig * (1.0 + gate_pre * (1.0 - gate_sig))).astype(
        jnp.bfloat16
    )
    pre_up = (hidden_grad * gate_pre * gate_sig).astype(jnp.bfloat16)
    pre_both = jnp.concatenate([pre_gate, pre_up], axis=1)
    grad_down = []
    grad_gate = []
    grad_up = []
    for q in range(pieces):
        grad_down.append(lax.dot_general(
            activated, rows_grad[q], token_contract, preferred_element_type=jnp.float32
        ).astype(jnp.bfloat16))
        grad_both = lax.dot_general(
            pre_both, rows_x[q], token_contract, preferred_element_type=jnp.float32
        ).astype(jnp.bfloat16)
        grad_gate.append(grad_both[:hidden])
        grad_up.append(grad_both[hidden:])
    grad_down = jnp.concatenate(grad_down, axis=1)
    grad_gate = jnp.concatenate(grad_gate, axis=1)
    grad_up = jnp.concatenate(grad_up, axis=1)
    back_pieces = 2
    back_width = model_width // back_pieces
    handed = []
    for q in range(back_pieces):
        cols = slice(q * back_width, (q + 1) * back_width)
        partial_in = jnp.dot(pre_both, both_mat[:, cols], preferred_element_type=jnp.float32)
        if q == 0:
            score_cols = jnp.pad(row_score[:, None], ((0, 0), (0, 127)))
            partial_in = jnp.concatenate([partial_in, score_cols], axis=1)
        summed = ring_reduce_scatter(partial_in.astype(jnp.bfloat16), "dp", my_group)
        span = capacity * back_width // 8
        body = summed[:, :back_width].reshape(experts, 8, span)
        if q == 0:
            tail = summed[:, back_width].reshape(experts, 1, capacity)
            tail = jnp.pad(tail, ((0, 0), (0, 7), (0, 128 - capacity)))
            body = jnp.concatenate([body, tail], axis=2)
        back = lax.all_to_all(body, "expert", 0, 0, tiled=True)
        if q == 0:
            slot_score = back[:, 0, span : span + capacity]
        flat_in = back[:, :, :span].reshape(experts * capacity, back_width)
        piece_grad = jnp.dot(table_half, flat_in, preferred_element_type=jnp.float32).astype(
            jnp.bfloat16
        )
        handed.append(from_behind(piece_grad, "pipe", -1))
    handed = jnp.concatenate(handed, axis=1)
    slot_score = slot_score.astype(jnp.float32).reshape(-1)
    picked = jnp.sum(jnp.where(table, slot_score[None, :], jnp.float32(0.0)), axis=1)
    gate_grad = picked / gate
    is_first = (jnp.arange(score_rows.shape[1]) == 0).astype(jnp.float32)
    score_grad = gate_grad[:, None] * weights[:, 0:1] * (is_first - weights)
    return (
        score_grad[None],
        handed[None],
        grad_gate[None, None],
        grad_up[None, None],
        grad_down[None, None],
    )


def solution(mesh):
    in_specs = (
        P("pipe", ("expert", "dp"), None),
        P("pipe", ("expert", "dp"), None),
        P("pipe", ("expert", "dp"), None),
        P("pipe", ("expert", "dp"), None),
        P("pipe", "expert", "dp", None),
        P("pipe", "expert", "dp", None),
        P("pipe", "expert", "dp", None),
    )
    out_specs = (
        P("pipe", ("expert", "dp"), None),
        P("pipe", ("expert", "dp"), None),
        P("pipe", "expert", "dp", None),
        P("pipe", "expert", "dp", None),
        P("pipe", "expert", "dp", None),
    )
    return jax.shard_map(
        per_device, mesh=mesh, in_specs=in_specs, out_specs=out_specs, check_vma=False
    )
```

```python
import jax
import jax.numpy as jnp
from jax import lax
from jax.sharding import PartitionSpec as P


def from_behind(shard, axis, by):
    length = lax.axis_size(axis)
    pairs = [(i, i + by) for i in range(length) if 0 <= i + by < length]
    return lax.ppermute(shard, axis, pairs)


def ring_gather(piece, axis, me):
    size = lax.axis_size(axis)
    rows = piece.shape[0]
    half = rows // 2
    fwd = [(k, (k + 1) % size) for k in range(size)]
    bwd = [(k, (k - 1) % size) for k in range(size)]
    from_left = lax.ppermute(piece, axis, fwd)
    from_right = lax.ppermute(piece, axis, bwd)
    far_top = lax.ppermute(from_left[:half], axis, fwd)
    far_bottom = lax.ppermute(from_right[half:], axis, bwd)
    far = jnp.concatenate([far_top, far_bottom], axis=0)
    return jnp.concatenate([piece, from_right, far, from_left], axis=0)


def ring_reduce_scatter(parts, axis, me):
    size = lax.axis_size(axis)
    rows = parts.shape[0] // size
    half = rows // 2
    fwd = [(k, (k + 1) % size) for k in range(size)]
    bwd = [(k, (k - 1) % size) for k in range(size)]

    def block(offset):
        return parts[offset * rows : (offset + 1) * rows]

    far = block(2)
    got_top = lax.ppermute(far[:half], axis, fwd)
    got_bottom = lax.ppermute(far[half:], axis, bwd)
    to_right = block(1).astype(jnp.float32)
    to_right = jnp.concatenate([to_right[:half] + got_top.astype(jnp.float32), to_right[half:]])
    to_left = block(size - 1).astype(jnp.float32)
    to_left = jnp.concatenate([to_left[:half], to_left[half:] + got_bottom.astype(jnp.float32)])
    from_left = lax.ppermute(to_right.astype(jnp.bfloat16), axis, fwd)
    from_right = lax.ppermute(to_left.astype(jnp.bfloat16), axis, bwd)
    total = block(0).astype(jnp.float32) + from_left.astype(jnp.float32)
    total = total + from_right.astype(jnp.float32)
    return total.astype(jnp.bfloat16)


def route_tables(route_col, score_rows, experts, capacity):
    expert_ids = jnp.arange(experts, dtype=jnp.int32)
    onehot = (route_col[:, None] == expert_ids).astype(jnp.int32)
    earlier = jnp.cumsum(onehot, axis=0) - onehot
    slot = jnp.sum(onehot * earlier, axis=1)
    position = route_col * capacity + slot
    raised = jnp.exp(score_rows)
    weights = raised / jnp.sum(raised, axis=1, keepdims=True)
    gate = lax.optimization_barrier(weights[:, 0].astype(jnp.bfloat16)).astype(jnp.float32)
    table = position[:, None] == jnp.arange(experts * capacity, dtype=jnp.int32)
    return (weights, gate, table)


def dense_chunks(rows, chunks):
    return rows.reshape(chunks, -1, 1024)


def per_device(inputs, routes, router_scores, cotangent, w_gate, w_up, w_down):
    tokens_in = inputs[0]
    upstream = cotangent[0]
    route_col = routes[0][:, 0]
    score_rows = router_scores[0]
    gate_mat = w_gate[0, 0]
    up_mat = w_up[0, 0]
    down_mat = w_down[0, 0]
    experts = lax.axis_size("expert")
    groups = lax.axis_size("dp")
    my_expert = lax.axis_index("expert")
    my_group = lax.axis_index("dp")
    token_count, model_width = tokens_in.shape
    capacity = max(2, token_count * 5 // (4 * experts))
    weights, gate, table = route_tables(route_col, score_rows, experts, capacity)
    table_half = table.astype(jnp.bfloat16)
    token_contract = (((0,), (0,)), ((), ()))
    feature_contract = (((1,), (1,)), ((), ()))
    scaled = (gate[:, None] * upstream.astype(jnp.float32)).astype(jnp.bfloat16)
    local_x = lax.dot_general(
        table_half, tokens_in, token_contract, preferred_element_type=jnp.float32
    ).astype(jnp.bfloat16)
    local_dy = lax.dot_general(
        table_half, scaled, token_contract, preferred_element_type=jnp.float32
    ).astype(jnp.bfloat16)
    pieces = 1
    width = model_width // pieces
    rows_x = []
    rows_grad = []
    for q in range(pieces):
        cols = slice(q * width, (q + 1) * width)
        x_e = lax.all_to_all(dense_chunks(local_x[:, cols], experts), "expert", 0, 0, tiled=True)
        x_e = x_e.reshape(experts * capacity, width)
        rows_x.append(ring_gather(x_e, "dp", my_group))
    for q in range(pieces):
        cols = slice(q * width, (q + 1) * width)
        dy_e = lax.all_to_all(dense_chunks(local_dy[:, cols], experts), "expert", 0, 0, tiled=True)
        dy_e = dy_e.reshape(experts * capacity, width)
        rows_grad.append(ring_gather(dy_e, "dp", my_group))
    both_mat = jnp.concatenate([gate_mat, up_mat], axis=0)
    hidden = gate_mat.shape[0]
    both_pre = 0.0
    for q in range(pieces):
        cols = slice(q * width, (q + 1) * width)
        both_pre = both_pre + lax.dot_general(
            rows_x[q], both_mat[:, cols], feature_contract, preferred_element_type=jnp.float32
        )
    gate_pre = both_pre[:, :hidden]
    up_pre = both_pre[:, hidden:]
    gate_sig = jax.nn.sigmoid(gate_pre)
    activated = (gate_pre * gate_sig * up_pre).astype(jnp.bfloat16)
    row_score = 0.0
    hidden_grad = 0.0
    for q in range(pieces):
        cols = slice(q * width, (q + 1) * width)
        partial_out = jnp.dot(activated, down_mat[:, cols], preferred_element_type=jnp.float32)
        row_score = row_score + jnp.sum(partial_out * rows_grad[q].astype(jnp.float32), axis=1)
        hidden_grad = hidden_grad + lax.dot_general(
            rows_grad[q], down_mat[:, cols], feature_contract, preferred_element_type=jnp.float32
        )
    pre_gate = (hidden_grad * up_pre * gate_sig * (1.0 + gate_pre * (1.0 - gate_sig))).astype(
        jnp.bfloat16
    )
    pre_up = (hidden_grad * gate_pre * gate_sig).astype(jnp.bfloat16)
    pre_both = jnp.concatenate([pre_gate, pre_up], axis=1)
    grad_down = []
    grad_gate = []
    grad_up = []
    for q in range(pieces):
        grad_down.append(lax.dot_general(
            activated, rows_grad[q], token_contract, preferred_element_type=jnp.float32
        ).astype(jnp.bfloat16))
        grad_both = lax.dot_general(
            pre_both, rows_x[q], token_contract, preferred_element_type=jnp.float32
        ).astype(jnp.bfloat16)
        grad_gate.append(grad_both[:hidden])
        grad_up.append(grad_both[hidden:])
    grad_down = jnp.concatenate(grad_down, axis=1)
    grad_gate = jnp.concatenate(grad_gate, axis=1)
    grad_up = jnp.concatenate(grad_up, axis=1)
    unit = model_width // 8
    back_widths = [5 * unit, 3 * unit]
    handed = []
    offset = 0
    for q, back_width in enumerate(back_widths):
        cols = slice(offset, offset + back_width)
        offset += back_width
        partial_in = jnp.dot(pre_both, both_mat[:, cols], preferred_element_type=jnp.float32)
        if q == 0:
            score_cols = jnp.pad(row_score[:, None], ((0, 0), (0, 127)))
            partial_in = jnp.concatenate([partial_in, score_cols], axis=1)
        summed = ring_reduce_scatter(partial_in.astype(jnp.bfloat16), "dp", my_group)
        span = capacity * back_width // 8
        body = summed[:, :back_width].reshape(experts, 8, span)
        if q == 0:
            tail = summed[:, back_width].reshape(experts, 1, capacity)
            tail = jnp.pad(tail, ((0, 0), (0, 7), (0, 128 - capacity)))
            body = jnp.concatenate([body, tail], axis=2)
        back = lax.all_to_all(body, "expert", 0, 0, tiled=True)
        if q == 0:
            slot_score = back[:, 0, span : span + capacity]
        flat_in = back[:, :, :span].reshape(experts * capacity, back_width)
        piece_grad = jnp.dot(table_half, flat_in, preferred_element_type=jnp.float32).astype(
            jnp.bfloat16
        )
        handed.append(from_behind(piece_grad, "pipe", -1))
    handed = jnp.concatenate(handed, axis=1)
    slot_score = slot_score.astype(jnp.float32).reshape(-1)
    picked = jnp.sum(jnp.where(table, slot_score[None, :], jnp.float32(0.0)), axis=1)
    gate_grad = picked / gate
    is_first = (jnp.arange(score_rows.shape[1]) == 0).astype(jnp.float32)
    score_grad = gate_grad[:, None] * weights[:, 0:1] * (is_first - weights)
    return (
        score_grad[None],
        handed[None],
        grad_gate[None, None],
        grad_up[None, None],
        grad_down[None, None],
    )


def solution(mesh):
    in_specs = (
        P("pipe", ("expert", "dp"), None),
        P("pipe", ("expert", "dp"), None),
        P("pipe", ("expert", "dp"), None),
        P("pipe", ("expert", "dp"), None),
        P("pipe", "expert", "dp", None),
        P("pipe", "expert", "dp", None),
        P("pipe", "expert", "dp", None),
    )
    out_specs = (
        P("pipe", ("expert", "dp"), None),
        P("pipe", ("expert", "dp"), None),
        P("pipe", "expert", "dp", None),
        P("pipe", "expert", "dp", None),
        P("pipe", "expert", "dp", None),
    )
    return jax.shard_map(
        per_device, mesh=mesh, in_specs=in_specs, out_specs=out_specs, check_vma=False
    )
```

```python
import jax
import jax.numpy as jnp
from jax import lax
from jax.sharding import PartitionSpec as P


def from_behind(shard, axis, by):
    length = lax.axis_size(axis)
    pairs = [(i, i + by) for i in range(length) if 0 <= i + by < length]
    return lax.ppermute(shard, axis, pairs)


def ring_gather(piece, axis, me):
    size = lax.axis_size(axis)
    rows = piece.shape[0]
    half = rows // 2
    fwd = [(k, (k + 1) % size) for k in range(size)]
    bwd = [(k, (k - 1) % size) for k in range(size)]
    from_left = lax.ppermute(piece, axis, fwd)
    from_right = lax.ppermute(piece, axis, bwd)
    far_top = lax.ppermute(from_left[:half], axis, fwd)
    far_bottom = lax.ppermute(from_right[half:], axis, bwd)
    far = jnp.concatenate([far_top, far_bottom], axis=0)
    return jnp.concatenate([piece, from_right, far, from_left], axis=0)


def ring_reduce_scatter(parts, axis, me):
    size = lax.axis_size(axis)
    rows = parts.shape[0] // size
    half = rows // 2
    fwd = [(k, (k + 1) % size) for k in range(size)]
    bwd = [(k, (k - 1) % size) for k in range(size)]

    def block(offset):
        return parts[offset * rows : (offset + 1) * rows]

    far = block(2)
    got_top = lax.ppermute(far[:half], axis, fwd)
    got_bottom = lax.ppermute(far[half:], axis, bwd)
    to_right = block(1).astype(jnp.float32)
    to_right = jnp.concatenate([to_right[:half] + got_top.astype(jnp.float32), to_right[half:]])
    to_left = block(size - 1).astype(jnp.float32)
    to_left = jnp.concatenate([to_left[:half], to_left[half:] + got_bottom.astype(jnp.float32)])
    from_left = lax.ppermute(to_right.astype(jnp.bfloat16), axis, fwd)
    from_right = lax.ppermute(to_left.astype(jnp.bfloat16), axis, bwd)
    total = block(0).astype(jnp.float32) + from_left.astype(jnp.float32)
    total = total + from_right.astype(jnp.float32)
    return total.astype(jnp.bfloat16)


def route_tables(route_col, score_rows, experts, capacity):
    expert_ids = jnp.arange(experts, dtype=jnp.int32)
    onehot = (route_col[:, None] == expert_ids).astype(jnp.int32)
    earlier = jnp.cumsum(onehot, axis=0) - onehot
    slot = jnp.sum(onehot * earlier, axis=1)
    position = route_col * capacity + slot
    raised = jnp.exp(score_rows)
    weights = raised / jnp.sum(raised, axis=1, keepdims=True)
    gate = lax.optimization_barrier(weights[:, 0].astype(jnp.bfloat16)).astype(jnp.float32)
    table = position[:, None] == jnp.arange(experts * capacity, dtype=jnp.int32)
    return (weights, gate, table)


def dense_chunks(rows, chunks):
    return rows.reshape(chunks, -1, 1024)


def per_device(inputs, routes, router_scores, cotangent, w_gate, w_up, w_down):
    tokens_in = inputs[0]
    upstream = cotangent[0]
    route_col = routes[0][:, 0]
    score_rows = router_scores[0]
    gate_mat = w_gate[0, 0]
    up_mat = w_up[0, 0]
    down_mat = w_down[0, 0]
    experts = lax.axis_size("expert")
    groups = lax.axis_size("dp")
    my_expert = lax.axis_index("expert")
    my_group = lax.axis_index("dp")
    token_count, model_width = tokens_in.shape
    capacity = max(2, token_count * 5 // (4 * experts))
    weights, gate, table = route_tables(route_col, score_rows, experts, capacity)
    table_half = table.astype(jnp.bfloat16)
    token_contract = (((0,), (0,)), ((), ()))
    feature_contract = (((1,), (1,)), ((), ()))
    scaled = (gate[:, None] * upstream.astype(jnp.float32)).astype(jnp.bfloat16)
    local_x = lax.dot_general(
        table_half, tokens_in, token_contract, preferred_element_type=jnp.float32
    ).astype(jnp.bfloat16)
    local_dy = lax.dot_general(
        table_half, scaled, token_contract, preferred_element_type=jnp.float32
    ).astype(jnp.bfloat16)
    pieces = 1
    width = model_width // pieces
    rows_x = []
    rows_grad = []
    for q in range(pieces):
        cols = slice(q * width, (q + 1) * width)
        x_e = lax.all_to_all(dense_chunks(local_x[:, cols], experts), "expert", 0, 0, tiled=True)
        x_e = x_e.reshape(experts * capacity, width)
        rows_x.append(ring_gather(x_e, "dp", my_group))
    for q in range(pieces):
        cols = slice(q * width, (q + 1) * width)
        dy_e = lax.all_to_all(dense_chunks(local_dy[:, cols], experts), "expert", 0, 0, tiled=True)
        dy_e = dy_e.reshape(experts * capacity, width)
        rows_grad.append(ring_gather(dy_e, "dp", my_group))
    both_mat = jnp.concatenate([gate_mat, up_mat], axis=0)
    hidden = gate_mat.shape[0]
    both_pre = 0.0
    for q in range(pieces):
        cols = slice(q * width, (q + 1) * width)
        both_pre = both_pre + lax.dot_general(
            rows_x[q], both_mat[:, cols], feature_contract, preferred_element_type=jnp.float32
        )
    gate_pre = both_pre[:, :hidden]
    up_pre = both_pre[:, hidden:]
    gate_sig = jax.nn.sigmoid(gate_pre)
    activated = (gate_pre * gate_sig * up_pre).astype(jnp.bfloat16)
    row_score = 0.0
    hidden_grad = 0.0
    for q in range(pieces):
        cols = slice(q * width, (q + 1) * width)
        partial_out = jnp.dot(activated, down_mat[:, cols], preferred_element_type=jnp.float32)
        row_score = row_score + jnp.sum(partial_out * rows_grad[q].astype(jnp.float32), axis=1)
        hidden_grad = hidden_grad + lax.dot_general(
            rows_grad[q], down_mat[:, cols], feature_contract, preferred_element_type=jnp.float32
        )
    pre_gate = (hidden_grad * up_pre * gate_sig * (1.0 + gate_pre * (1.0 - gate_sig))).astype(
        jnp.bfloat16
    )
    pre_up = (hidden_grad * gate_pre * gate_sig).astype(jnp.bfloat16)
    pre_both = jnp.concatenate([pre_gate, pre_up], axis=1)
    grad_down = []
    grad_gate = []
    grad_up = []
    for q in range(pieces):
        grad_down.append(lax.dot_general(
            activated, rows_grad[q], token_contract, preferred_element_type=jnp.float32
        ).astype(jnp.bfloat16))
        grad_both = lax.dot_general(
            pre_both, rows_x[q], token_contract, preferred_element_type=jnp.float32
        ).astype(jnp.bfloat16)
        grad_gate.append(grad_both[:hidden])
        grad_up.append(grad_both[hidden:])
    grad_down = jnp.concatenate(grad_down, axis=1)
    grad_gate = jnp.concatenate(grad_gate, axis=1)
    grad_up = jnp.concatenate(grad_up, axis=1)
    unit = model_width // 8
    back_widths = [6 * unit, 2 * unit]
    handed = []
    offset = 0
    for q, back_width in enumerate(back_widths):
        cols = slice(offset, offset + back_width)
        offset += back_width
        partial_in = jnp.dot(pre_both, both_mat[:, cols], preferred_element_type=jnp.float32)
        if q == 0:
            score_cols = jnp.pad(row_score[:, None], ((0, 0), (0, 127)))
            partial_in = jnp.concatenate([partial_in, score_cols], axis=1)
        summed = ring_reduce_scatter(partial_in.astype(jnp.bfloat16), "dp", my_group)
        span = capacity * back_width // 8
        body = summed[:, :back_width].reshape(experts, 8, span)
        if q == 0:
            tail = summed[:, back_width].reshape(experts, 1, capacity)
            tail = jnp.pad(tail, ((0, 0), (0, 7), (0, 128 - capacity)))
            body = jnp.concatenate([body, tail], axis=2)
        back = lax.all_to_all(body, "expert", 0, 0, tiled=True)
        if q == 0:
            slot_score = back[:, 0, span : span + capacity]
        flat_in = back[:, :, :span].reshape(experts * capacity, back_width)
        piece_grad = jnp.dot(table_half, flat_in, preferred_element_type=jnp.float32).astype(
            jnp.bfloat16
        )
        handed.append(from_behind(piece_grad, "pipe", -1))
    handed = jnp.concatenate(handed, axis=1)
    slot_score = slot_score.astype(jnp.float32).reshape(-1)
    picked = jnp.sum(jnp.where(table, slot_score[None, :], jnp.float32(0.0)), axis=1)
    gate_grad = picked / gate
    is_first = (jnp.arange(score_rows.shape[1]) == 0).astype(jnp.float32)
    score_grad = gate_grad[:, None] * weights[:, 0:1] * (is_first - weights)
    return (
        score_grad[None],
        handed[None],
        grad_gate[None, None],
        grad_up[None, None],
        grad_down[None, None],
    )


def solution(mesh):
    in_specs = (
        P("pipe", ("expert", "dp"), None),
        P("pipe", ("expert", "dp"), None),
        P("pipe", ("expert", "dp"), None),
        P("pipe", ("expert", "dp"), None),
        P("pipe", "expert", "dp", None),
        P("pipe", "expert", "dp", None),
        P("pipe", "expert", "dp", None),
    )
    out_specs = (
        P("pipe", ("expert", "dp"), None),
        P("pipe", ("expert", "dp"), None),
        P("pipe", "expert", "dp", None),
        P("pipe", "expert", "dp", None),
        P("pipe", "expert", "dp", None),
    )
    return jax.shard_map(
        per_device, mesh=mesh, in_specs=in_specs, out_specs=out_specs, check_vma=False
    )
```
